256 devices in a mesh: section: 2 (over core), shard: 128 (over z, x, y).
Axes of the slice: x: 4, y: 4, z: 8, core: 2. Of those that a mesh axis runs over, the one named last changes fastest.
Arguments:
- hidden: bfloat16 [512, 32, 768], P('shard', None, 'section'), may hold values from -6 to 6
- proj: bfloat16 [768, 128], P('section'), may hold values from -0.21875 to 0.21875
- passages: bfloat16 [16384, 180, 128], P('shard'), may hold values from -24 to 24
- pass_len: int32 [16384], P('shard'), may hold values from 45 to 180
- query_len: int32 [512], P('shard'), may hold values from 8 to 32
- cand_owner: int32 [2, 512, 32, 1], P('section', 'shard'), may hold values from 0 to 127; in each aligned block of 128 rows (0 to 127, 128 to 255, ..., all dimensions but the last counted through in order) at most 2 rows name the same one
- cand_slot: int32 [2, 512, 32], P('section', 'shard'), may hold values from 0 to 127
- teacher: float32 [512, 64], P('shard', 'section'), may hold values from -18 to 318
Outputs:
- kl_div: float32 [512], P('shard')
- grad_hidden: bfloat16 [512, 32, 768], P('shard', None, 'section')
- grad_proj: float32 [768, 128], P('section')
The draws below stay inside these ranges and needn't reach their ends.
Inputs may be any that keep to these rules, and one draw needn't show every extreme that they name: `cand_owner`: among the 128 candidates held by one device (one index of section, the queries of one index of shard), at most 2 name any one owner.
All inputs are finite; a program needn't handle non-finite values.
Results may differ from the reference program's by a relative error of at most 0.022.
Values may be sent and summed in bfloat16 or wider, within the bound.
No kernel may reach another device: no remote copies, remote signals or barrier semaphores. Data moves between devices by JAX's collectives and lax.ppermute only.
A program may use at most 128 MiB of HBM per device.

```python
import math
import jax
import jax.numpy as jnp
import numpy as np
from jax import lax

D = 768
DV = 128
QLEN = 32
PLEN = 180
NCAND = 64
CHIPQ = 4
PS = 128
HALF = 32
CAP = 2
QUERIES = 512
PASSAGES = 16384
N_SECTION = 2
N_SHARD = 128


def draw_passages(key, part):
    first = jax.random.fold_in(key, 0)
    base = jnp.clip(jax.random.normal(first, (PASSAGES, PLEN, DV), jnp.float32), -6.0, 6.0)
    return base.astype(jnp.bfloat16)


def draw_teacher(key, part):
    first, second = jax.random.split(key)
    offsets = jax.random.uniform(first, (QUERIES, 1), jnp.float32, 0.0, 50.0)
    noise = jnp.clip(jax.random.normal(second, (QUERIES, NCAND), jnp.float32), -6.0, 6.0) * 3.0
    return offsets + noise


def set_ends(drawn, own_key, least, high):
    longest = drawn.shape.index(max(drawn.shape))
    spots = []
    for shift in (0, 1):
        where = [jax.random.randint(jax.random.fold_in(own_key, axis), (), 0, length) for axis, length in enumerate(drawn.shape)]
        where[longest] = (where[longest] + shift) % drawn.shape[longest]
        spots.append(tuple(where))
    return drawn.at[spots[0]].set(least).at[spots[1]].set(high)


def block_levels(key, extent, cuts, low, top_value):
    level = 1.0
    for axis_at, parts in cuts:
        draws = jax.random.uniform(jax.random.fold_in(jax.random.fold_in(key, 6), axis_at), (parts,), jnp.float32, low / len(cuts), top_value / len(cuts))
        level = level * jnp.repeat(jnp.exp(draws), extent[axis_at] // parts).reshape((-1,) + (1,) * (len(extent) - 1 - axis_at))
    return level


def assign_block(own_key, own, number, rows, amount, top, limit, lean):
    ranking = jax.random.permutation(own_key, amount)
    packed, usual = load_shares(amount, rows * top, limit, lean, True), load_shares(amount, rows * top, limit, lean, False)
    places = jnp.arange(amount)

    def named(lengths, turn):
        used = int((lengths > 0).sum())
        fixed = max(1, used // 4)
        shifted = fixed + (places - fixed + turn * (used - fixed)) % max(1, amount - fixed)
        return jnp.zeros((amount,), jnp.int32).at[ranking[jnp.where(places < fixed, places, shifted)]].set(jnp.asarray(lengths, jnp.int32))

    lengths = jnp.where(number % 4 == 0, named(packed, number // 4), named(usual, number - number // 4 - 1))
    mixed = jax.random.permutation(jax.random.fold_in(own, 3), amount)
    source_of, sink = mixed[0:amount // 2 * 2:2], mixed[1:amount // 2 * 2:2]
    room = jnp.minimum(lengths[source_of] - 1, limit - lengths[sink]) // 2
    room = jnp.where((source_of == ranking[0]) | (sink == ranking[0]) | (lengths[sink] == 0), 0, jnp.maximum(room, 0))
    shifted = jax.random.randint(jax.random.fold_in(own, 4), (amount // 2,), 0, 1 << 20) % (room + 1)
    lengths = lengths.at[source_of].add(-shifted).at[sink].add(shifted)
    items = jnp.searchsorted(jnp.cumsum(lengths), jnp.arange(rows * top), side="right").astype(jnp.int32)
    table = items.reshape(top, rows).T
    table = table[jax.random.permutation(jax.random.fold_in(own, 1), rows)]
    turn = jax.random.randint(jax.random.fold_in(own, 2), (rows, 1), 0, top)
    return jnp.take_along_axis(table, (jnp.arange(top)[None, :] + turn) % top, axis=1)


def load_shares(number_of, total, limit, lean, full):
    weights = [(1 << 20) // math.isqrt(standing ** lean) + 1 for standing in range(1, number_of + 1)]
    largest = limit if full else min(limit, max(-(-total // number_of), total * weights[0] // sum(weights)))
    least = 1 if total - largest >= number_of - 1 else 0
    counts, surplus = [largest] + [least] * (number_of - 1), total - largest - least * (number_of - 1)
    while surplus > 0:
        free = [i for i in range(1, number_of) if counts[i] < largest] or [i for i in range(1, number_of) if counts[i] < limit]
        whole, budget = sum([weights[i] for i in free]), surplus
        for i in free:
            more = min(limit - counts[i], max(1, budget * weights[i] // whole), surplus)
            counts[i] = counts[i] + more
            surplus = surplus - more
    return np.array(counts)


def centred(stream_key, shape, scale, reach, pieces=(), kind=jnp.bfloat16):
    loudness = block_levels(stream_key, shape, pieces, -0.22, 0.18) if pieces else 1.0
    entries = jax.random.normal(stream_key, shape, jnp.float32) * scale * loudness
    return jnp.minimum(jnp.maximum(entries, -reach), reach).astype(kind)


def setup_inputs(seed: int = 0) -> dict:
    arg_keys = jax.random.split(jax.random.key(seed), 9)
    hidden = centred(arg_keys[0], (QUERIES, QLEN, D), 1.0, 6.0, ((0, 128), (2, 2)))
    proj = centred(arg_keys[1], (D, DV), D ** -0.5, 0.21875, ((0, 2),))
    passages = draw_passages(jax.random.fold_in(arg_keys[8], 71), 0)
    pass_len = set_ends(jax.random.randint(arg_keys[3], (PASSAGES,), PLEN // 4, PLEN + 1), jax.random.fold_in(arg_keys[3], 1), PLEN // 4, PLEN).astype(jnp.int32)
    query_len = set_ends(jax.random.randint(arg_keys[4], (QUERIES,), QLEN // 4, QLEN + 1), jax.random.fold_in(arg_keys[4], 1), QLEN // 4, QLEN).astype(jnp.int32)
    cand_owner_keys = jax.random.split(jax.random.fold_in(arg_keys[5], 1), N_SECTION * QUERIES * HALF // (CHIPQ * HALF))
    cand_owner_turns = jax.random.permutation(jax.random.fold_in(arg_keys[5], 3), N_SECTION * QUERIES * HALF // (CHIPQ * HALF))
    cand_owner = jax.vmap(lambda own, number: assign_block(jax.random.fold_in(arg_keys[5], 2), own, number, CHIPQ * HALF, N_SHARD, 1, CAP, 2))(cand_owner_keys, cand_owner_turns).reshape((N_SECTION, QUERIES, HALF, 1))
    cand_slot = set_ends(jax.random.randint(arg_keys[6], (N_SECTION, QUERIES, HALF), 0, PS), jax.random.fold_in(arg_keys[6], 1), 0, PS - 1).astype(jnp.int32)
    teacher = draw_teacher(jax.random.fold_in(arg_keys[8], 71), 0)
    return dict(hidden=hidden, proj=proj, passages=passages, pass_len=pass_len, query_len=query_len, cand_owner=cand_owner, cand_slot=cand_slot, teacher=teacher)


SHARPNESS = 64.0
EPSILON = 1e-06
NEGATIVE = -1e+30

def one_query(q_vecs, cand_ids, tok_mask, t_score, passages, pass_len):
    blocks = passages[cand_ids]
    cand_lens = pass_len[cand_ids]
    logits = jnp.einsum('id,ktd->kit', q_vecs.astype(jnp.float32), blocks.astype(jnp.float32)) * SHARPNESS
    in_range = jnp.arange(blocks.shape[1])[None, None, :] < cand_lens[:, None, None]
    logits = jnp.where(in_range, logits, NEGATIVE)
    top_logit = lax.optimization_barrier(jnp.max(logits, axis=2, keepdims=True))
    expo_terms = jnp.where(in_range, jnp.exp(logits - top_logit), 0.0)
    total = lax.optimization_barrier(jnp.sum(expo_terms, axis=2, keepdims=True))
    token_max = (top_logit[..., 0] + jnp.log(total[..., 0])) / SHARPNESS
    token_weight = expo_terms / total
    student = lax.optimization_barrier(jnp.sum(jnp.where(tok_mask[None, :], token_max, 0.0), axis=1))
    teach_top = jnp.max(t_score)
    lse_teach = teach_top + jnp.log(jnp.sum(jnp.exp(t_score - teach_top)))
    stud_top = jnp.max(student)
    lse_stud = stud_top + jnp.log(jnp.sum(jnp.exp(student - stud_top)))
    kl_div = jnp.sum(jnp.exp(t_score - lse_teach) * (t_score - student)) - lse_teach + lse_stud
    score_grad = jnp.exp(student - lse_stud) - jnp.exp(t_score - lse_teach)
    mixed = jnp.where(tok_mask[None, :, None], score_grad[:, None, None] * token_weight, 0.0).astype(jnp.bfloat16)
    vec_grad = jnp.einsum('kit,ktd->id', mixed.astype(jnp.float32), blocks.astype(jnp.float32))
    return (kl_div, vec_grad)

def reference(hidden, proj, passages, pass_len, query_len, cand_owner, cand_slot, teacher):
    num_queries, num_tokens, feat_width = hidden.shape
    vec_dim = proj.shape[1]
    flat_h = hidden.reshape(num_queries * num_tokens, feat_width)
    proj_in = jnp.dot(flat_h, proj, preferred_element_type=jnp.float32).reshape(num_queries, num_tokens, vec_dim)
    inv_norm = lax.rsqrt(lax.optimization_barrier(jnp.sum(proj_in * proj_in, axis=2, keepdims=True)) + EPSILON)
    query_vecs = (proj_in * inv_norm).astype(jnp.bfloat16)
    cand_ids = cand_owner[..., 0] * PS + cand_slot
    cand_ids = jnp.transpose(cand_ids, (1, 0, 2)).reshape(num_queries, NCAND).astype(jnp.int32)
    tok_mask = jnp.arange(num_tokens)[None, :] < query_len[:, None]

    def per_query(inputs_q):
        return one_query(inputs_q[0], inputs_q[1], inputs_q[2], inputs_q[3], passages, pass_len)
    kl_div, vec_grad = lax.map(per_query, (query_vecs, cand_ids, tok_mask, teacher))
    cubed = inv_norm * inv_norm * inv_norm
    in_grad = inv_norm * vec_grad - cubed * proj_in * lax.optimization_barrier(jnp.sum(proj_in * vec_grad, axis=2, keepdims=True))
    flat_in = in_grad.astype(jnp.bfloat16).reshape(num_queries * num_tokens, vec_dim)
    grad_hidden = jnp.dot(flat_in, proj.T, preferred_element_type=jnp.float32).astype(jnp.bfloat16)
    grad_hidden = grad_hidden.reshape(num_queries, num_tokens, feat_width)
    grad_proj = jnp.dot(flat_h.T, flat_in, preferred_element_type=jnp.float32)
    return (kl_div, grad_hidden, grad_proj)
```

```python
import jax
import jax.numpy as jnp
from jax import lax
from jax.sharding import PartitionSpec as P

SHARPNESS = 64.0
EPSILON = 1e-06
NEGATIVE = -1e30


def combined_all(value, axis, join):
    pieces = jax.tree.map(lambda part: lax.all_gather(part, axis), value)
    head = jax.tree.map(lambda part: part[0], pieces)
    tail = jax.tree.map(lambda part: part[1:], pieces)
    running, _ = lax.scan(lambda running, section: (join(running, section), None), head, tail)
    return running


def token_scores(q_rows, blocks, cand_lens):
    logits = (
        jnp.einsum("bid,btd->bit", q_rows, blocks, preferred_element_type=jnp.float32) * SHARPNESS
    )
    in_range = jnp.arange(blocks.shape[1])[None, None, :] < cand_lens[:, None, None]
    logits = jnp.where(in_range, logits, NEGATIVE)
    top_logit = jnp.max(logits, axis=2, keepdims=True)
    expo_terms = jnp.where(in_range, jnp.exp(logits - top_logit), 0.0)
    total = jnp.sum(expo_terms, axis=2, keepdims=True)
    token_max = (top_logit[..., 0] + jnp.log(total[..., 0])) / SHARPNESS
    return (token_max, expo_terms / total)


def merge_halves(first, second):
    teach_top = jnp.maximum(first[0], second[0])
    scale_one = jnp.exp(first[0] - teach_top)
    scale_two = jnp.exp(second[0] - teach_top)
    stud_top = jnp.maximum(first[3], second[3])
    fact_one = jnp.exp(first[3] - stud_top)
    fact_two = jnp.exp(second[3] - stud_top)
    return (
        teach_top,
        first[1] * scale_one + second[1] * scale_two,
        first[2] * scale_one + second[2] * scale_two,
        stud_top,
        first[4] * fact_one + second[4] * fact_two,
    )


def pair_sum(value):
    return value + lax.ppermute(value, "section", [(0, 1), (1, 0)])


def spread_sum(value, axis, size):
    pieces = value.reshape(size, -1, value.shape[-1])
    summed = lax.all_to_all(pieces, axis, 0, 0, tiled=True).sum(axis=0)
    spread = jnp.broadcast_to(summed[None], pieces.shape)
    return lax.all_to_all(spread, axis, 0, 0, tiled=True).reshape(value.shape)


def local(hidden, proj, passages, pass_len, query_len, cand_owner, cand_slot, teacher):
    num_queries, num_tokens, feat_half = hidden.shape
    vec_dim = proj.shape[1]
    pass_tokens = passages.shape[1]
    owners = lax.axis_size("shard")
    flat_h = hidden.reshape(num_queries * num_tokens, feat_half)
    partial_in = jnp.dot(flat_h, proj, preferred_element_type=jnp.float32).reshape(
        num_queries, num_tokens, vec_dim
    )
    proj_in = pair_sum(partial_in)
    inv_norm = lax.rsqrt(jnp.sum(proj_in * proj_in, axis=2, keepdims=True) + EPSILON)
    query_vecs = (proj_in * inv_norm).astype(jnp.bfloat16)
    tok_mask = jnp.arange(num_tokens)[None, :] < query_len[:, None]
    owner_ids = cand_owner.reshape(-1)
    slot_ids = cand_slot.reshape(-1)
    requests = owner_ids.shape[0]
    cand_half = requests // num_queries
    capacity = max(2, (2 * requests + owners - 1) // owners)
    onehot = (owner_ids[:, None] == jnp.arange(owners)[None, :]).astype(jnp.int32)
    rank_ids = jnp.sum((jnp.cumsum(onehot, axis=0) - onehot) * onehot, axis=1)
    buf_pos = owner_ids * capacity + rank_ids
    query_of = jnp.arange(requests) // cand_half
    req_mask = tok_mask[query_of]
    slot_table = jnp.zeros((owners, capacity), jnp.int32).at[owner_ids, rank_ids].set(slot_ids)
    wanted = lax.all_to_all(slot_table, "shard", split_axis=0, concat_axis=0, tiled=True).reshape(
        -1
    )
    out_blocks = passages[wanted].reshape(owners, capacity, pass_tokens, vec_dim)
    out_lens = pass_len[wanted].reshape(owners, capacity)
    got_blocks, got_lens = (
        lax.all_to_all(out_blocks, "shard", split_axis=0, concat_axis=0, tiled=True),
        lax.all_to_all(out_lens, "shard", split_axis=0, concat_axis=0, tiled=True),
    )
    blocks = got_blocks.reshape(owners * capacity, pass_tokens, vec_dim)[buf_pos]
    cand_lens = got_lens.reshape(-1)[buf_pos]
    token_max, weight = token_scores(query_vecs[query_of], blocks, cand_lens)
    student = jnp.sum(jnp.where(req_mask, token_max, 0.0), axis=1).reshape(num_queries, cand_half)
    teach_top = jnp.max(teacher, axis=1)
    teach_exp = jnp.exp(teacher - teach_top[:, None])
    teach_sum = jnp.sum(teach_exp, axis=1)
    teach_wsum = jnp.sum(teach_exp * (teacher - student), axis=1)
    stud_top = jnp.max(student, axis=1)
    stud_sum = jnp.sum(jnp.exp(student - stud_top[:, None]), axis=1)
    top_teach, sum_teach, wsum_teach, top_stud, sum_stud = combined_all(
        (teach_top, teach_sum, teach_wsum, stud_top, stud_sum), "section", merge_halves
    )
    lse_teach = top_teach + jnp.log(sum_teach)
    lse_stud = top_stud + jnp.log(sum_stud)
    kl_div = wsum_teach / sum_teach - lse_teach + lse_stud
    score_grad = jnp.exp(student - lse_stud[:, None]) - jnp.exp(teacher - lse_teach[:, None])
    flat_grad = score_grad.reshape(-1)
    mixed = jnp.where(req_mask[:, :, None], flat_grad[:, None, None] * weight, 0.0).astype(
        jnp.bfloat16
    )
    part_grad = jnp.einsum("bit,btd->bid", mixed, blocks, preferred_element_type=jnp.float32)
    half_grad = jnp.sum(part_grad.reshape(num_queries, cand_half, num_tokens, vec_dim), axis=1)
    vec_grad = pair_sum(half_grad)
    cubed = inv_norm * inv_norm * inv_norm
    in_grad = inv_norm * vec_grad - cubed * proj_in * jnp.sum(
        proj_in * vec_grad, axis=2, keepdims=True
    )
    flat_in = in_grad.astype(jnp.bfloat16).reshape(num_queries * num_tokens, vec_dim)
    grad_hidden = jnp.dot(flat_in, proj.T, preferred_element_type=jnp.float32).astype(jnp.bfloat16)
    grad_hidden = grad_hidden.reshape(num_queries, num_tokens, feat_half)
    local_proj = jnp.dot(flat_h.T, flat_in, preferred_element_type=jnp.float32)
    grad_proj = spread_sum(local_proj, "shard", owners)
    return (kl_div, grad_hidden, grad_proj)


def solution(mesh):
    in_specs = (
        P("shard", None, "section"),
        P("section", None),
        P("shard", None, None),
        P("shard"),
        P("shard"),
        P("section", "shard", None, None),
        P("section", "shard", None),
        P("shard", "section"),
    )
    out_specs = (P("shard"), P("shard", None, "section"), P("section", None))
    return jax.shard_map(local, mesh=mesh, in_specs=in_specs, out_specs=out_specs, check_vma=False)
```

```python
import jax
import jax.numpy as jnp
from jax import lax
from jax.sharding import PartitionSpec as P

SHARPNESS = 64.0
EPSILON = 1e-06
NEGATIVE = -1e30
CAPACITY = 2


def combined_all(value, axis, join):
    pieces = jax.tree.map(lambda part: lax.all_gather(part, axis), value)
    head = jax.tree.map(lambda part: part[0], pieces)
    tail = jax.tree.map(lambda part: part[1:], pieces)
    running, _ = lax.scan(lambda running, section: (join(running, section), None), head, tail)
    return running


def token_scores(q_rows, blocks, cand_lens):
    logits = (
        jnp.einsum("bid,btd->bit", q_rows, blocks, preferred_element_type=jnp.float32) * SHARPNESS
    )
    in_range = jnp.arange(blocks.shape[1])[None, None, :] < cand_lens[:, None, None]
    logits = jnp.where(in_range, logits, NEGATIVE)
    top_logit = jnp.max(logits, axis=2, keepdims=True)
    expo_terms = jnp.where(in_range, jnp.exp(logits - top_logit), 0.0)
    total = jnp.sum(expo_terms, axis=2, keepdims=True)
    token_max = (top_logit[..., 0] + jnp.log(total[..., 0])) / SHARPNESS
    return (token_max, expo_terms / total)


def merge_halves(first, second):
    teach_top = jnp.maximum(first[0], second[0])
    scale_one = jnp.exp(first[0] - teach_top)
    scale_two = jnp.exp(second[0] - teach_top)
    stud_top = jnp.maximum(first[3], second[3])
    fact_one = jnp.exp(first[3] - stud_top)
    fact_two = jnp.exp(second[3] - stud_top)
    return (
        teach_top,
        first[1] * scale_one + second[1] * scale_two,
        first[2] * scale_one + second[2] * scale_two,
        stud_top,
        first[4] * fact_one + second[4] * fact_two,
    )


def pair_sum(value):
    return value + lax.ppermute(value, "section", [(0, 1), (1, 0)])


def spread_sum(value, axis, size):
    pieces = value.reshape(size, -1, value.shape[-1])
    summed = lax.all_to_all(pieces, axis, 0, 0, tiled=True).sum(axis=0)
    spread = jnp.broadcast_to(summed[None], pieces.shape)
    return lax.all_to_all(spread, axis, 0, 0, tiled=True).reshape(value.shape)


def split_three(value):
    high = lax.reduce_precision(value, exponent_bits=8, mantissa_bits=7)
    rest = value - high
    middle = lax.reduce_precision(rest, exponent_bits=8, mantissa_bits=7)
    return high, middle, rest - middle


def lane_row(width, entries):
    lane = jnp.arange(width)[None, :]
    row = jnp.zeros((entries[0].shape[0], width), jnp.float32)
    for place, entry in enumerate(entries):
        row = jnp.where(lane == place, entry.astype(jnp.float32)[:, None], row)
    return row.astype(jnp.bfloat16)


def local(hidden, proj, passages, pass_len, query_len, cand_owner, cand_slot, teacher):
    num_queries, num_tokens, feat_half = hidden.shape
    vec_dim = proj.shape[1]
    held, pass_tokens = passages.shape[0], passages.shape[1]
    owners = lax.axis_size("shard")
    flat_h = hidden.reshape(num_queries * num_tokens, feat_half)
    partial_in = jnp.dot(flat_h, proj, preferred_element_type=jnp.float32).reshape(
        num_queries, num_tokens, vec_dim
    )
    proj_in = pair_sum(partial_in)
    inv_norm = lax.rsqrt(jnp.sum(proj_in * proj_in, axis=2, keepdims=True) + EPSILON)
    query_vecs = (proj_in * inv_norm).astype(jnp.bfloat16)
    tok_mask = jnp.arange(num_tokens)[None, :] < query_len[:, None]
    owner_ids = cand_owner.reshape(-1)
    slot_ids = cand_slot.reshape(-1)
    requests = owner_ids.shape[0]
    cand_half = requests // num_queries
    capacity = CAPACITY
    slots = owners * capacity
    onehot = (owner_ids[:, None] == jnp.arange(owners)[None, :]).astype(jnp.int32)
    rank_ids = jnp.sum((jnp.cumsum(onehot, axis=0) - onehot) * onehot, axis=1)
    buf_pos = owner_ids * capacity + rank_ids
    query_of = jnp.arange(requests) // cand_half
    pick = buf_pos[None, :] == jnp.arange(slots)[:, None]
    slot_query = jnp.any(pick[:, :, None] & (query_of[:, None] == jnp.arange(num_queries))[None], axis=1)
    row = num_tokens * vec_dim
    q_send = jnp.dot(
        slot_query.astype(jnp.bfloat16),
        query_vecs.reshape(num_queries, row),
        preferred_element_type=jnp.float32,
    ).astype(jnp.bfloat16)
    slot_meta = jnp.sum(jnp.where(pick, slot_ids[None, :], 0), axis=1)
    qlen_meta = jnp.sum(jnp.where(pick, query_len[query_of][None, :], 0), axis=1)
    width = row + vec_dim
    payload = jnp.concatenate([q_send, lane_row(vec_dim, (slot_meta, qlen_meta))], axis=1)
    recv = lax.all_to_all(
        payload.reshape(owners, capacity * width), "shard", 0, 0, tiled=True
    ).reshape(slots, width)
    q_rows = recv[:, :row].reshape(slots, num_tokens, vec_dim)
    slot_at = recv[:, row].astype(jnp.int32)
    qlen_at = recv[:, row + 1].astype(jnp.int32)
    choose = slot_at[:, None] == jnp.arange(held)[None, :]
    blocks = (
        jnp.dot(
            choose.astype(jnp.bfloat16),
            passages.reshape(held, pass_tokens * vec_dim),
            preferred_element_type=jnp.float32,
        )
        .astype(jnp.bfloat16)
        .reshape(slots, pass_tokens, vec_dim)
    )
    cand_lens = jnp.sum(jnp.where(choose, pass_len[None, :], 0), axis=1)
    token_max, weight = token_scores(q_rows, blocks, cand_lens)
    stud_at = jnp.sum(
        jnp.where(jnp.arange(num_tokens)[None, :] < qlen_at[:, None], token_max, 0.0), axis=1
    )
    pulled = jnp.einsum(
        "bit,btd->bid", weight.astype(jnp.bfloat16), blocks, preferred_element_type=jnp.float32
    )
    back = jnp.concatenate(
        [pulled.astype(jnp.bfloat16).reshape(slots, row), lane_row(vec_dim, split_three(stud_at))],
        axis=1,
    )
    got = lax.all_to_all(
        back.reshape(owners, capacity * width), "shard", 0, 0, tiled=True
    ).reshape(slots, width)
    mine = jnp.dot(pick.T.astype(jnp.bfloat16), got, preferred_element_type=jnp.float32)
    student = ((mine[:, row] + mine[:, row + 1]) + mine[:, row + 2]).reshape(num_queries, cand_half)
    pulled_mine = mine[:, :row].reshape(num_queries, cand_half, num_tokens, vec_dim)
    teach_top = jnp.max(teacher, axis=1)
    teach_exp = jnp.exp(teacher - teach_top[:, None])
    teach_sum = jnp.sum(teach_exp, axis=1)
    teach_wsum = jnp.sum(teach_exp * (teacher - student), axis=1)
    stud_top = jnp.max(student, axis=1)
    stud_sum = jnp.sum(jnp.exp(student - stud_top[:, None]), axis=1)
    top_teach, sum_teach, wsum_teach, top_stud, sum_stud = combined_all(
        (teach_top, teach_sum, teach_wsum, stud_top, stud_sum), "section", merge_halves
    )
    lse_teach = top_teach + jnp.log(sum_teach)
    lse_stud = top_stud + jnp.log(sum_stud)
    kl_div = wsum_teach / sum_teach - lse_teach + lse_stud
    score_grad = jnp.exp(student - lse_stud[:, None]) - jnp.exp(teacher - lse_teach[:, None])
    half_grad = jnp.sum(score_grad[:, :, None, None] * pulled_mine, axis=1)
    half_grad = jnp.where(tok_mask[:, :, None], half_grad, 0.0)
    vec_grad = pair_sum(half_grad)
    cubed = inv_norm * inv_norm * inv_norm
    in_grad = inv_norm * vec_grad - cubed * proj_in * jnp.sum(
        proj_in * vec_grad, axis=2, keepdims=True
    )
    flat_in = in_grad.astype(jnp.bfloat16).reshape(num_queries * num_tokens, vec_dim)
    grad_hidden = jnp.dot(flat_in, proj.T, preferred_element_type=jnp.float32).astype(jnp.bfloat16)
    grad_hidden = grad_hidden.reshape(num_queries, num_tokens, feat_half)
    local_proj = jnp.dot(flat_h.T, flat_in, preferred_element_type=jnp.float32)
    grad_proj = spread_sum(local_proj, "shard", owners)
    return (kl_div, grad_hidden, grad_proj)


def solution(mesh):
    in_specs = (
        P("shard", None, "section"),
        P("section", None),
        P("shard", None, None),
        P("shard"),
        P("shard"),
        P("section", "shard", None, None),
        P("section", "shard", None),
        P("shard", "section"),
    )
    out_specs = (P("shard"), P("shard", None, "section"), P("section", None))
    return jax.shard_map(local, mesh=mesh, in_specs=in_specs, out_specs=out_specs, check_vma=False)
```

```python
import jax
import jax.numpy as jnp
from jax import lax
from jax.sharding import PartitionSpec as P

SHARPNESS = 64.0
EPSILON = 1e-06
NEGATIVE = -1e30
CAPACITY = 2


def combined_all(value, axis, join):
    pieces = jax.tree.map(lambda part: lax.all_gather(part, axis), value)
    head = jax.tree.map(lambda part: part[0], pieces)
    tail = jax.tree.map(lambda part: part[1:], pieces)
    running, _ = lax.scan(lambda running, section: (join(running, section), None), head, tail)
    return running


def token_scores(q_rows, blocks, cand_lens):
    logits = (
        jnp.einsum("bid,btd->bit", q_rows, blocks, preferred_element_type=jnp.float32) * SHARPNESS
    )
    in_range = jnp.arange(blocks.shape[1])[None, None, :] < cand_lens[:, None, None]
    logits = jnp.where(in_range, logits, NEGATIVE)
    top_logit = jnp.max(logits, axis=2, keepdims=True)
    expo_terms = jnp.where(in_range, jnp.exp(logits - top_logit), 0.0)
    total = jnp.sum(expo_terms, axis=2, keepdims=True)
    token_max = (top_logit[..., 0] + jnp.log(total[..., 0])) / SHARPNESS
    return (token_max, expo_terms / total)


def merge_halves(first, second):
    teach_top = jnp.maximum(first[0], second[0])
    scale_one = jnp.exp(first[0] - teach_top)
    scale_two = jnp.exp(second[0] - teach_top)
    stud_top = jnp.maximum(first[3], second[3])
    fact_one = jnp.exp(first[3] - stud_top)
    fact_two = jnp.exp(second[3] - stud_top)
    return (
        teach_top,
        first[1] * scale_one + second[1] * scale_two,
        first[2] * scale_one + second[2] * scale_two,
        stud_top,
        first[4] * fact_one + second[4] * fact_two,
    )


def pair_sum(value):
    return value + lax.ppermute(value, "section", [(0, 1), (1, 0)])


def spread_sum(value, axis, size):
    pieces = value.reshape(size, -1, value.shape[-1])
    summed = lax.all_to_all(pieces, axis, 0, 0, tiled=True).sum(axis=0)
    spread = jnp.broadcast_to(summed[None], pieces.shape)
    return lax.all_to_all(spread, axis, 0, 0, tiled=True).reshape(value.shape)


def split_three(value):
    high = lax.reduce_precision(value, exponent_bits=8, mantissa_bits=7)
    rest = value - high
    middle = lax.reduce_precision(rest, exponent_bits=8, mantissa_bits=7)
    return high, middle, rest - middle


def lane_row(width, entries):
    lane = jnp.arange(width)[None, :]
    row = jnp.zeros((entries[0].shape[0], width), jnp.float32)
    for place, entry in enumerate(entries):
        spots = entry.shape[1]
        for spot in range(spots):
            row = jnp.where(lane == place * spots + spot, entry[:, spot : spot + 1].astype(jnp.float32), row)
    return row.astype(jnp.bfloat16)[:, None, :]


def local(hidden, proj, passages, pass_len, query_len, cand_owner, cand_slot, teacher):
    num_queries, num_tokens, feat_half = hidden.shape
    vec_dim = proj.shape[1]
    held = passages.shape[0]
    owners = lax.axis_size("shard")
    flat_h = hidden.reshape(num_queries * num_tokens, feat_half)
    partial_in = jnp.dot(flat_h, proj, preferred_element_type=jnp.float32).reshape(
        num_queries, num_tokens, vec_dim
    )
    proj_in = pair_sum(partial_in)
    inv_norm = lax.rsqrt(jnp.sum(proj_in * proj_in, axis=2, keepdims=True) + EPSILON)
    query_vecs = (proj_in * inv_norm).astype(jnp.bfloat16)
    tok_mask = jnp.arange(num_tokens)[None, :] < query_len[:, None]
    owner_ids = cand_owner.reshape(-1)
    slot_ids = cand_slot.reshape(-1)
    requests = owner_ids.shape[0]
    cand_half = requests // num_queries
    capacity = CAPACITY
    slots = owners * capacity
    onehot = (owner_ids[:, None] == jnp.arange(owners)[None, :]).astype(jnp.int32)
    rank_ids = jnp.sum((jnp.cumsum(onehot, axis=0) - onehot) * onehot, axis=1)
    buf_pos = owner_ids * capacity + rank_ids
    query_of = jnp.arange(requests) // cand_half
    pick = buf_pos[None, :] == jnp.arange(slots)[:, None]
    slot_query = jnp.any(pick[:, :, None] & (query_of[:, None] == jnp.arange(num_queries))[None], axis=1)
    q_send = jnp.einsum(
        "sq,qid->sid", slot_query.astype(jnp.bfloat16), query_vecs, preferred_element_type=jnp.float32
    ).astype(jnp.bfloat16)
    slot_meta = jnp.sum(jnp.where(pick, slot_ids[None, :], 0), axis=1).reshape(owners, capacity)
    qlen_meta = jnp.sum(jnp.where(pick, query_len[query_of][None, :], 0), axis=1).reshape(owners, capacity)
    body = capacity * num_tokens
    payload = jnp.concatenate(
        [q_send.reshape(owners, body, vec_dim), lane_row(vec_dim, (slot_meta, qlen_meta))], axis=1
    )
    recv = lax.all_to_all(payload, "shard", 0, 0, tiled=True)
    q_rows = recv[:, :body, :].reshape(slots, num_tokens, vec_dim)
    slot_at = recv[:, body, :capacity].astype(jnp.int32).reshape(slots)
    qlen_at = recv[:, body, capacity : 2 * capacity].astype(jnp.int32).reshape(slots)
    choose = slot_at[:, None] == jnp.arange(held)[None, :]
    blocks = jnp.einsum(
        "sp,ptd->std", choose.astype(jnp.bfloat16), passages, preferred_element_type=jnp.float32
    ).astype(jnp.bfloat16)
    cand_lens = jnp.sum(jnp.where(choose, pass_len[None, :], 0), axis=1)
    token_max, weight = token_scores(q_rows, blocks, cand_lens)
    stud_at = jnp.sum(
        jnp.where(jnp.arange(num_tokens)[None, :] < qlen_at[:, None], token_max, 0.0), axis=1
    )
    pulled = jnp.einsum(
        "bit,btd->bid", weight.astype(jnp.bfloat16), blocks, preferred_element_type=jnp.float32
    )
    pieces = tuple(piece.reshape(owners, capacity) for piece in split_three(stud_at))
    back = jnp.concatenate(
        [pulled.astype(jnp.bfloat16).reshape(owners, body, vec_dim), lane_row(vec_dim, pieces)], axis=1
    )
    got = lax.all_to_all(back, "shard", 0, 0, tiled=True)
    got_pulled = got[:, :body, :].reshape(slots, num_tokens, vec_dim)
    take = pick.T.astype(jnp.bfloat16)
    mine = jnp.einsum("rs,sid->rid", take, got_pulled, preferred_element_type=jnp.float32)
    got_meta = got[:, body, : 3 * capacity].astype(jnp.float32).reshape(owners, 3, capacity)
    got_meta = jnp.transpose(got_meta, (1, 0, 2)).reshape(3, slots)
    parts = jnp.sum(jnp.where(pick[None], got_meta[:, :, None], 0.0), axis=1)
    student = ((parts[0] + parts[1]) + parts[2]).reshape(num_queries, cand_half)
    pulled_mine = mine.reshape(num_queries, cand_half, num_tokens, vec_dim)
    teach_top = jnp.max(teacher, axis=1)
    teach_exp = jnp.exp(teacher - teach_top[:, None])
    teach_sum = jnp.sum(teach_exp, axis=1)
    teach_wsum = jnp.sum(teach_exp * (teacher - student), axis=1)
    stud_top = jnp.max(student, axis=1)
    stud_sum = jnp.sum(jnp.exp(student - stud_top[:, None]), axis=1)
    top_teach, sum_teach, wsum_teach, top_stud, sum_stud = combined_all(
        (teach_top, teach_sum, teach_wsum, stud_top, stud_sum), "section", merge_halves
    )
    lse_teach = top_teach + jnp.log(sum_teach)
    lse_stud = top_stud + jnp.log(sum_stud)
    kl_div = wsum_teach / sum_teach - lse_teach + lse_stud
    score_grad = jnp.exp(student - lse_stud[:, None]) - jnp.exp(teacher - lse_teach[:, None])
    half_grad = jnp.sum(score_grad[:, :, None, None] * pulled_mine, axis=1)
    half_grad = jnp.where(tok_mask[:, :, None], half_grad, 0.0)
    vec_grad = pair_sum(half_grad)
    cubed = inv_norm * inv_norm * inv_norm
    in_grad = inv_norm * vec_grad - cubed * proj_in * jnp.sum(
        proj_in * vec_grad, axis=2, keepdims=True
    )
    flat_in = in_grad.astype(jnp.bfloat16).reshape(num_queries * num_tokens, vec_dim)
    grad_hidden = jnp.dot(flat_in, proj.T, preferred_element_type=jnp.float32).astype(jnp.bfloat16)
    grad_hidden = grad_hidden.reshape(num_queries, num_tokens, feat_half)
    local_proj = jnp.dot(flat_h.T, flat_in, preferred_element_type=jnp.float32)
    grad_proj = spread_sum(local_proj, "shard", owners)
    return (kl_div, grad_hidden, grad_proj)


def solution(mesh):
    in_specs = (
        P("shard", None, "section"),
        P("section", None),
        P("shard", None, None),
        P("shard"),
        P("shard"),
        P("section", "shard", None, None),
        P("section", "shard", None),
        P("shard", "section"),
    )
    out_specs = (P("shard"), P("shard", None, "section"), P("section", None))
    return jax.shard_map(local, mesh=mesh, in_specs=in_specs, out_specs=out_specs, check_vma=False)
```

```python
import jax
import jax.numpy as jnp
from jax import lax
from jax.sharding import PartitionSpec as P
from jax.experimental import pallas as pl
from jax.experimental.pallas import tpu as pltpu

SHARPNESS = 64.0
EPSILON = 1e-06
NEGATIVE = -1e30
CAPACITY = 2
GROUP = 8


def combined_all(value, axis, join):
    pieces = jax.tree.map(lambda part: lax.all_gather(part, axis), value)
    head = jax.tree.map(lambda part: part[0], pieces)
    tail = jax.tree.map(lambda part: part[1:], pieces)
    running, _ = lax.scan(lambda running, section: (join(running, section), None), head, tail)
    return running


def token_scores(q_rows, blocks, cand_lens):
    logits = (
        jnp.einsum("bid,btd->bit", q_rows, blocks, preferred_element_type=jnp.float32) * SHARPNESS
    )
    in_range = jnp.arange(blocks.shape[1])[None, None, :] < cand_lens[:, None, None]
    logits = jnp.where(in_range, logits, NEGATIVE)
    top_logit = jnp.max(logits, axis=2, keepdims=True)
    expo_terms = jnp.where(in_range, jnp.exp(logits - top_logit), 0.0)
    total = jnp.sum(expo_terms, axis=2, keepdims=True)
    token_max = (top_logit[..., 0] + jnp.log(total[..., 0])) / SHARPNESS
    return (token_max, expo_terms / total)


def merge_halves(first, second):
    teach_top = jnp.maximum(first[0], second[0])
    scale_one = jnp.exp(first[0] - teach_top)
    scale_two = jnp.exp(second[0] - teach_top)
    stud_top = jnp.maximum(first[3], second[3])
    fact_one = jnp.exp(first[3] - stud_top)
    fact_two = jnp.exp(second[3] - stud_top)
    return (
        teach_top,
        first[1] * scale_one + second[1] * scale_two,
        first[2] * scale_one + second[2] * scale_two,
        stud_top,
        first[4] * fact_one + second[4] * fact_two,
    )


def pair_sum(value):
    return value + lax.ppermute(value, "section", [(0, 1), (1, 0)])


def spread_sum(value, axis, size):
    pieces = value.reshape(size, -1, value.shape[-1])
    summed = lax.all_to_all(pieces, axis, 0, 0, tiled=True).sum(axis=0)
    spread = jnp.broadcast_to(summed[None], pieces.shape)
    return lax.all_to_all(spread, axis, 0, 0, tiled=True).reshape(value.shape)


def split_three(value):
    high = lax.reduce_precision(value, exponent_bits=8, mantissa_bits=7)
    rest = value - high
    middle = lax.reduce_precision(rest, exponent_bits=8, mantissa_bits=7)
    return high, middle, rest - middle


def lane_row(width, entries):
    lane = jnp.arange(width)[None, :]
    row = jnp.zeros((entries[0].shape[0], width), jnp.float32)
    for place, entry in enumerate(entries):
        spots = entry.shape[1]
        for spot in range(spots):
            row = jnp.where(lane == place * spots + spot, entry[:, spot : spot + 1].astype(jnp.float32), row)
    return row.astype(jnp.bfloat16)[:, None, :]


def score_kernel(slot_ref, qlen_ref, len_ref, q_ref, p_ref, pt_ref, pulled_ref, stud_ref):
    group, num_tokens, _ = q_ref.shape
    pass_tokens = p_ref.shape[1]
    base = pl.program_id(0) * group
    for spot in range(group):
        slot = slot_ref[base + spot]
        limit = len_ref[slot]
        logits = (
            lax.dot_general(
                p_ref[slot], q_ref[spot], (((1,), (1,)), ((), ())), preferred_element_type=jnp.float32
            )
            * SHARPNESS
        )
        in_range = lax.broadcasted_iota(jnp.int32, (pass_tokens, num_tokens), 0) < limit
        logits = jnp.where(in_range, logits, NEGATIVE)
        top_logit = jnp.max(logits, axis=0, keepdims=True)
        expo_terms = jnp.where(in_range, jnp.exp(logits - top_logit), 0.0)
        total = jnp.sum(expo_terms, axis=0, keepdims=True)
        token_max = (top_logit + jnp.log(total)) / SHARPNESS
        weight = (expo_terms / total).astype(jnp.bfloat16)
        pulled = jnp.dot(pt_ref[slot], weight, preferred_element_type=jnp.float32)
        pulled_ref[spot] = pulled.T.astype(jnp.bfloat16)
        cols = lax.broadcasted_iota(jnp.int32, (1, num_tokens), 1)
        score = jnp.sum(jnp.where(cols < qlen_ref[base + spot], token_max, 0.0))
        stud_ref[pl.ds(spot, 1), :] = jnp.full((1, stud_ref.shape[1]), score, jnp.float32)


def owner_scores(q_rows, passages, slot_at, qlen_at, pass_len):
    slots, num_tokens, vec_dim = q_rows.shape
    held, pass_tokens, _ = passages.shape
    group = GROUP
    grid_spec = pltpu.PrefetchScalarGridSpec(
        num_scalar_prefetch=3,
        grid=(slots // group,),
        in_specs=[
            pl.BlockSpec((group, num_tokens, vec_dim), lambda i, *_: (i, 0, 0)),
            pl.BlockSpec((held, pass_tokens, vec_dim), lambda i, *_: (0, 0, 0)),
            pl.BlockSpec((held, vec_dim, pass_tokens), lambda i, *_: (0, 0, 0)),
        ],
        out_specs=[
            pl.BlockSpec((group, num_tokens, vec_dim), lambda i, *_: (i, 0, 0)),
            pl.BlockSpec((group, 128), lambda i, *_: (i, 0)),
        ],
    )
    flops = 4 * slots * num_tokens * pass_tokens * vec_dim
    moved = 2 * (2 * held * pass_tokens * vec_dim + 2 * slots * num_tokens * vec_dim)
    return pl.pallas_call(
        score_kernel,
        grid_spec=grid_spec,
        out_shape=[
            jax.ShapeDtypeStruct((slots, num_tokens, vec_dim), jnp.bfloat16),
            jax.ShapeDtypeStruct((slots, 128), jnp.float32),
        ],
        compiler_params=pltpu.CompilerParams(vmem_limit_bytes=60 * 1024 * 1024),
        cost_estimate=pl.CostEstimate(
            flops=flops, transcendentals=slots * num_tokens * pass_tokens, bytes_accessed=moved
        ),
    )(slot_at, qlen_at, pass_len, q_rows, passages, jnp.swapaxes(passages, 1, 2))


def local(hidden, proj, passages, pass_len, query_len, cand_owner, cand_slot, teacher):
    num_queries, num_tokens, feat_half = hidden.shape
    vec_dim = proj.shape[1]
    held = passages.shape[0]
    owners = lax.axis_size("shard")
    flat_h = hidden.reshape(num_queries * num_tokens, feat_half)
    partial_in = jnp.dot(flat_h, proj, preferred_element_type=jnp.float32).reshape(
        num_queries, num_tokens, vec_dim
    )
    proj_in = pair_sum(partial_in)
    inv_norm = lax.rsqrt(jnp.sum(proj_in * proj_in, axis=2, keepdims=True) + EPSILON)
    query_vecs = (proj_in * inv_norm).astype(jnp.bfloat16)
    tok_mask = jnp.arange(num_tokens)[None, :] < query_len[:, None]
    owner_ids = cand_owner.reshape(-1)
    slot_ids = cand_slot.reshape(-1)
    requests = owner_ids.shape[0]
    cand_half = requests // num_queries
    capacity = CAPACITY
    slots = owners * capacity
    onehot = (owner_ids[:, None] == jnp.arange(owners)[None, :]).astype(jnp.int32)
    rank_ids = jnp.sum((jnp.cumsum(onehot, axis=0) - onehot) * onehot, axis=1)
    buf_pos = owner_ids * capacity + rank_ids
    query_of = jnp.arange(requests) // cand_half
    pick = buf_pos[None, :] == jnp.arange(slots)[:, None]
    slot_query = jnp.any(pick[:, :, None] & (query_of[:, None] == jnp.arange(num_queries))[None], axis=1)
    q_send = jnp.einsum(
        "sq,qid->sid", slot_query.astype(jnp.bfloat16), query_vecs, preferred_element_type=jnp.float32
    ).astype(jnp.bfloat16)
    slot_meta = jnp.sum(jnp.where(pick, slot_ids[None, :], 0), axis=1).reshape(owners, capacity)
    qlen_meta = jnp.sum(jnp.where(pick, query_len[query_of][None, :], 0), axis=1).reshape(owners, capacity)
    body = capacity * num_tokens
    payload = jnp.concatenate(
        [q_send.reshape(owners, body, vec_dim), lane_row(vec_dim, (slot_meta, qlen_meta))], axis=1
    )
    recv = lax.all_to_all(payload, "shard", 0, 0, tiled=True)
    q_rows = recv[:, :body, :].reshape(slots, num_tokens, vec_dim)
    slot_at = recv[:, body, :capacity].astype(jnp.int32).reshape(slots)
    qlen_at = recv[:, body, capacity : 2 * capacity].astype(jnp.int32).reshape(slots)
    pulled, stud_rows = owner_scores(q_rows, passages, slot_at, qlen_at, pass_len)
    stud_at = stud_rows[:, 0]
    pieces = tuple(piece.reshape(owners, capacity) for piece in split_three(stud_at))
    back = jnp.concatenate(
        [pulled.reshape(owners, body, vec_dim), lane_row(vec_dim, pieces)], axis=1
    )
    got = lax.all_to_all(back, "shard", 0, 0, tiled=True)
    got_pulled = got[:, :body, :].reshape(slots, num_tokens, vec_dim)
    take = pick.T.astype(jnp.bfloat16)
    mine = jnp.einsum("rs,sid->rid", take, got_pulled, preferred_element_type=jnp.float32)
    got_meta = got[:, body, : 3 * capacity].astype(jnp.float32).reshape(owners, 3, capacity)
    got_meta = jnp.transpose(got_meta, (1, 0, 2)).reshape(3, slots)
    parts = jnp.sum(jnp.where(pick[None], got_meta[:, :, None], 0.0), axis=1)
    student = ((parts[0] + parts[1]) + parts[2]).reshape(num_queries, cand_half)
    pulled_mine = mine.reshape(num_queries, cand_half, num_tokens, vec_dim)
    teach_top = jnp.max(teacher, axis=1)
    teach_exp = jnp.exp(teacher - teach_top[:, None])
    teach_sum = jnp.sum(teach_exp, axis=1)
    teach_wsum = jnp.sum(teach_exp * (teacher - student), axis=1)
    stud_top = jnp.max(student, axis=1)
    stud_sum = jnp.sum(jnp.exp(student - stud_top[:, None]), axis=1)
    top_teach, sum_teach, wsum_teach, top_stud, sum_stud = combined_all(
        (teach_top, teach_sum, teach_wsum, stud_top, stud_sum), "section", merge_halves
    )
    lse_teach = top_teach + jnp.log(sum_teach)
    lse_stud = top_stud + jnp.log(sum_stud)
    kl_div = wsum_teach / sum_teach - lse_teach + lse_stud
    score_grad = jnp.exp(student - lse_stud[:, None]) - jnp.exp(teacher - lse_teach[:, None])
    half_grad = jnp.sum(score_grad[:, :, None, None] * pulled_mine, axis=1)
    half_grad = jnp.where(tok_mask[:, :, None], half_grad, 0.0)
    vec_grad = pair_sum(half_grad)
    cubed = inv_norm * inv_norm * inv_norm
    in_grad = inv_norm * vec_grad - cubed * proj_in * jnp.sum(
        proj_in * vec_grad, axis=2, keepdims=True
    )
    flat_in = in_grad.astype(jnp.bfloat16).reshape(num_queries * num_tokens, vec_dim)
    grad_hidden = jnp.dot(flat_in, proj.T, preferred_element_type=jnp.float32).astype(jnp.bfloat16)
    grad_hidden = grad_hidden.reshape(num_queries, num_tokens, feat_half)
    local_proj = jnp.dot(flat_h.T, flat_in, preferred_element_type=jnp.float32)
    grad_proj = spread_sum(local_proj, "shard", owners)
    return (kl_div, grad_hidden, grad_proj)


def solution(mesh):
    in_specs = (
        P("shard", None, "section"),
        P("section", None),
        P("shard", None, None),
        P("shard"),
        P("shard"),
        P("section", "shard", None, None),
        P("section", "shard", None),
        P("shard", "section"),
    )
    out_specs = (P("shard"), P("shard", None, "section"), P("section", None))
    return jax.shard_map(local, mesh=mesh, in_specs=in_specs, out_specs=out_specs, check_vma=False)
```

```python
import jax
import jax.numpy as jnp
from jax import lax
from jax.sharding import PartitionSpec as P
from jax.experimental import pallas as pl
from jax.experimental.pallas import tpu as pltpu

SHARPNESS = 64.0
EPSILON = 1e-06
NEGATIVE = -1e30
CAPACITY = 2
GROUP = 8


def combined_all(value, axis, join):
    pieces = jax.tree.map(lambda part: lax.all_gather(part, axis), value)
    head = jax.tree.map(lambda part: part[0], pieces)
    tail = jax.tree.map(lambda part: part[1:], pieces)
    running, _ = lax.scan(lambda running, section: (join(running, section), None), head, tail)
    return running


def token_scores(q_rows, blocks, cand_lens):
    logits = (
        jnp.einsum("bid,btd->bit", q_rows, blocks, preferred_element_type=jnp.float32) * SHARPNESS
    )
    in_range = jnp.arange(blocks.shape[1])[None, None, :] < cand_lens[:, None, None]
    logits = jnp.where(in_range, logits, NEGATIVE)
    top_logit = jnp.max(logits, axis=2, keepdims=True)
    expo_terms = jnp.where(in_range, jnp.exp(logits - top_logit), 0.0)
    total = jnp.sum(expo_terms, axis=2, keepdims=True)
    token_max = (top_logit[..., 0] + jnp.log(total[..., 0])) / SHARPNESS
    return (token_max, expo_terms / total)


def merge_halves(first, second):
    teach_top = jnp.maximum(first[0], second[0])
    scale_one = jnp.exp(first[0] - teach_top)
    scale_two = jnp.exp(second[0] - teach_top)
    stud_top = jnp.maximum(first[3], second[3])
    fact_one = jnp.exp(first[3] - stud_top)
    fact_two = jnp.exp(second[3] - stud_top)
    return (
        teach_top,
        first[1] * scale_one + second[1] * scale_two,
        first[2] * scale_one + second[2] * scale_two,
        stud_top,
        first[4] * fact_one + second[4] * fact_two,
    )


def pair_sum(value):
    return value + lax.ppermute(value, "section", [(0, 1), (1, 0)])


def spread_sum(value, axis, size):
    pieces = value.reshape(size, -1, value.shape[-1])
    summed = lax.all_to_all(pieces, axis, 0, 0, tiled=True).sum(axis=0)
    spread = jnp.broadcast_to(summed[None], pieces.shape)
    return lax.all_to_all(spread, axis, 0, 0, tiled=True).reshape(value.shape)


def split_three(value):
    high = lax.reduce_precision(value, exponent_bits=8, mantissa_bits=7)
    rest = value - high
    middle = lax.reduce_precision(rest, exponent_bits=8, mantissa_bits=7)
    return high, middle, rest - middle


def lane_row(width, entries):
    lane = jnp.arange(width)[None, :]
    row = jnp.zeros((entries[0].shape[0], width), jnp.float32)
    for place, entry in enumerate(entries):
        spots = entry.shape[1]
        for spot in range(spots):
            row = jnp.where(lane == place * spots + spot, entry[:, spot : spot + 1].astype(jnp.float32), row)
    return row.astype(jnp.bfloat16)[:, None, :]


def score_kernel(slot_ref, qlen_ref, len_ref, q_ref, p_ref, pt_ref, pulled_ref, stud_ref):
    group, num_tokens, vec_dim = q_ref.shape
    pass_tokens = p_ref.shape[1]
    base = pl.program_id(0) * group
    for spot in range(group):
        used = qlen_ref[base + spot] > 0

        @pl.when(used)
        def _score(spot=spot):
            slot = slot_ref[base + spot]
            limit = len_ref[slot]
            logits = (
                lax.dot_general(
                    p_ref[slot],
                    q_ref[spot],
                    (((1,), (1,)), ((), ())),
                    preferred_element_type=jnp.float32,
                )
                * SHARPNESS
            )
            in_range = lax.broadcasted_iota(jnp.int32, (pass_tokens, num_tokens), 0) < limit
            logits = jnp.where(in_range, logits, NEGATIVE)
            top_logit = jnp.max(logits, axis=0, keepdims=True)
            expo_terms = jnp.where(in_range, jnp.exp(logits - top_logit), 0.0)
            total = jnp.sum(expo_terms, axis=0, keepdims=True)
            token_max = (top_logit + jnp.log(total)) / SHARPNESS
            weight = (expo_terms / total).astype(jnp.bfloat16)
            pulled = jnp.dot(pt_ref[slot], weight, preferred_element_type=jnp.float32)
            pulled_ref[spot] = pulled.T.astype(jnp.bfloat16)
            cols = lax.broadcasted_iota(jnp.int32, (1, num_tokens), 1)
            score = jnp.sum(jnp.where(cols < qlen_ref[base + spot], token_max, 0.0))
            stud_ref[pl.ds(spot, 1), :] = jnp.full((1, stud_ref.shape[1]), score, jnp.float32)

        @pl.when(jnp.logical_not(used))
        def _empty(spot=spot):
            pulled_ref[spot] = jnp.zeros((num_tokens, vec_dim), jnp.bfloat16)
            stud_ref[pl.ds(spot, 1), :] = jnp.zeros((1, stud_ref.shape[1]), jnp.float32)


def owner_scores(q_rows, passages, slot_at, qlen_at, pass_len):
    slots, num_tokens, vec_dim = q_rows.shape
    held, pass_tokens, _ = passages.shape
    group = GROUP
    grid_spec = pltpu.PrefetchScalarGridSpec(
        num_scalar_prefetch=3,
        grid=(slots // group,),
        in_specs=[
            pl.BlockSpec((group, num_tokens, vec_dim), lambda i, *_: (i, 0, 0)),
            pl.BlockSpec((held, pass_tokens, vec_dim), lambda i, *_: (0, 0, 0)),
            pl.BlockSpec((held, vec_dim, pass_tokens), lambda i, *_: (0, 0, 0)),
        ],
        out_specs=[
            pl.BlockSpec((group, num_tokens, vec_dim), lambda i, *_: (i, 0, 0)),
            pl.BlockSpec((group, 128), lambda i, *_: (i, 0)),
        ],
    )
    flops = 4 * slots * num_tokens * pass_tokens * vec_dim
    moved = 2 * (2 * held * pass_tokens * vec_dim + 2 * slots * num_tokens * vec_dim)
    return pl.pallas_call(
        score_kernel,
        grid_spec=grid_spec,
        out_shape=[
            jax.ShapeDtypeStruct((slots, num_tokens, vec_dim), jnp.bfloat16),
            jax.ShapeDtypeStruct((slots, 128), jnp.float32),
        ],
        compiler_params=pltpu.CompilerParams(vmem_limit_bytes=60 * 1024 * 1024),
        cost_estimate=pl.CostEstimate(
            flops=flops, transcendentals=slots * num_tokens * pass_tokens, bytes_accessed=moved
        ),
    )(slot_at, qlen_at, pass_len, q_rows, passages, jnp.swapaxes(passages, 1, 2))


def local(hidden, proj, passages, pass_len, query_len, cand_owner, cand_slot, teacher):
    num_queries, num_tokens, feat_half = hidden.shape
    vec_dim = proj.shape[1]
    held = passages.shape[0]
    owners = lax.axis_size("shard")
    flat_h = hidden.reshape(num_queries * num_tokens, feat_half)
    partial_in = jnp.dot(flat_h, proj, preferred_element_type=jnp.float32).reshape(
        num_queries, num_tokens, vec_dim
    )
    proj_in = pair_sum(partial_in)
    inv_norm = lax.rsqrt(jnp.sum(proj_in * proj_in, axis=2, keepdims=True) + EPSILON)
    query_vecs = (proj_in * inv_norm).astype(jnp.bfloat16)
    tok_mask = jnp.arange(num_tokens)[None, :] < query_len[:, None]
    owner_ids = cand_owner.reshape(-1)
    slot_ids = cand_slot.reshape(-1)
    requests = owner_ids.shape[0]
    cand_half = requests // num_queries
    capacity = CAPACITY
    slots = owners * capacity
    onehot = (owner_ids[:, None] == jnp.arange(owners)[None, :]).astype(jnp.int32)
    rank_ids = jnp.sum((jnp.cumsum(onehot, axis=0) - onehot) * onehot, axis=1)
    buf_pos = owner_ids * capacity + rank_ids
    query_of = jnp.arange(requests) // cand_half
    pick = buf_pos[None, :] == jnp.arange(slots)[:, None]
    slot_query = jnp.any(pick[:, :, None] & (query_of[:, None] == jnp.arange(num_queries))[None], axis=1)
    q_send = jnp.einsum(
        "sq,qid->sid", slot_query.astype(jnp.bfloat16), query_vecs, preferred_element_type=jnp.float32
    ).astype(jnp.bfloat16)
    slot_meta = jnp.sum(jnp.where(pick, slot_ids[None, :], 0), axis=1).reshape(owners, capacity)
    qlen_meta = jnp.sum(jnp.where(pick, query_len[query_of][None, :], 0), axis=1).reshape(owners, capacity)
    body = capacity * num_tokens
    payload = jnp.concatenate(
        [q_send.reshape(owners, body, vec_dim), lane_row(vec_dim, (slot_meta, qlen_meta))], axis=1
    )
    recv = lax.all_to_all(payload, "shard", 0, 0, tiled=True)
    q_rows = recv[:, :body, :].reshape(slots, num_tokens, vec_dim)
    slot_at = recv[:, body, :capacity].astype(jnp.int32).reshape(slots)
    qlen_at = recv[:, body, capacity : 2 * capacity].astype(jnp.int32).reshape(slots)
    pulled, stud_rows = owner_scores(q_rows, passages, slot_at, qlen_at, pass_len)
    stud_at = stud_rows[:, 0]
    pieces = tuple(piece.reshape(owners, capacity) for piece in split_three(stud_at))
    back = jnp.concatenate(
        [pulled.reshape(owners, body, vec_dim), lane_row(vec_dim, pieces)], axis=1
    )
    got = lax.all_to_all(back, "shard", 0, 0, tiled=True)
    got_pulled = got[:, :body, :].reshape(slots, num_tokens, vec_dim)
    take = pick.T.astype(jnp.bfloat16)
    mine = jnp.einsum("rs,sid->rid", take, got_pulled, preferred_element_type=jnp.float32)
    got_meta = got[:, body, : 3 * capacity].astype(jnp.float32).reshape(owners, 3, capacity)
    got_meta = jnp.transpose(got_meta, (1, 0, 2)).reshape(3, slots)
    parts = jnp.sum(jnp.where(pick[None], got_meta[:, :, None], 0.0), axis=1)
    student = ((parts[0] + parts[1]) + parts[2]).reshape(num_queries, cand_half)
    pulled_mine = mine.reshape(num_queries, cand_half, num_tokens, vec_dim)
    teach_top = jnp.max(teacher, axis=1)
    teach_exp = jnp.exp(teacher - teach_top[:, None])
    teach_sum = jnp.sum(teach_exp, axis=1)
    teach_wsum = jnp.sum(teach_exp * (teacher - student), axis=1)
    stud_top = jnp.max(student, axis=1)
    stud_sum = jnp.sum(jnp.exp(student - stud_top[:, None]), axis=1)
    top_teach, sum_teach, wsum_teach, top_stud, sum_stud = combined_all(
        (teach_top, teach_sum, teach_wsum, stud_top, stud_sum), "section", merge_halves
    )
    lse_teach = top_teach + jnp.log(sum_teach)
    lse_stud = top_stud + jnp.log(sum_stud)
    kl_div = wsum_teach / sum_teach - lse_teach + lse_stud
    score_grad = jnp.exp(student - lse_stud[:, None]) - jnp.exp(teacher - lse_teach[:, None])
    half_grad = jnp.sum(score_grad[:, :, None, None] * pulled_mine, axis=1)
    half_grad = jnp.where(tok_mask[:, :, None], half_grad, 0.0)
    vec_grad = pair_sum(half_grad)
    cubed = inv_norm * inv_norm * inv_norm
    in_grad = inv_norm * vec_grad - cubed * proj_in * jnp.sum(
        proj_in * vec_grad, axis=2, keepdims=True
    )
    flat_in = in_grad.astype(jnp.bfloat16).reshape(num_queries * num_tokens, vec_dim)
    grad_hidden = jnp.dot(flat_in, proj.T, preferred_element_type=jnp.float32).astype(jnp.bfloat16)
    grad_hidden = grad_hidden.reshape(num_queries, num_tokens, feat_half)
    local_proj = jnp.dot(flat_h.T, flat_in, preferred_element_type=jnp.float32)
    grad_proj = spread_sum(local_proj, "shard", owners)
    return (kl_div, grad_hidden, grad_proj)


def solution(mesh):
    in_specs = (
        P("shard", None, "section"),
        P("section", None),
        P("shard", None, None),
        P("shard"),
        P("shard"),
        P("section", "shard", None, None),
        P("section", "shard", None),
        P("shard", "section"),
    )
    out_specs = (P("shard"), P("shard", None, "section"), P("section", None))
    return jax.shard_map(local, mesh=mesh, in_specs=in_specs, out_specs=out_specs, check_vma=False)
```

```python
import jax
import jax.numpy as jnp
from jax import lax
from jax.sharding import PartitionSpec as P
from jax.experimental import pallas as pl
from jax.experimental.pallas import tpu as pltpu

SHARPNESS = 64.0
EPSILON = 1e-06
NEGATIVE = -1e30
CAPACITY = 2
GROUP = 16


def combined_all(value, axis, join):
    pieces = jax.tree.map(lambda part: lax.all_gather(part, axis), value)
    head = jax.tree.map(lambda part: part[0], pieces)
    tail = jax.tree.map(lambda part: part[1:], pieces)
    running, _ = lax.scan(lambda running, section: (join(running, section), None), head, tail)
    return running


def token_scores(q_rows, blocks, cand_lens):
    logits = (
        jnp.einsum("bid,btd->bit", q_rows, blocks, preferred_element_type=jnp.float32) * SHARPNESS
    )
    in_range = jnp.arange(blocks.shape[1])[None, None, :] < cand_lens[:, None, None]
    logits = jnp.where(in_range, logits, NEGATIVE)
    top_logit = jnp.max(logits, axis=2, keepdims=True)
    expo_terms = jnp.where(in_range, jnp.exp(logits - top_logit), 0.0)
    total = jnp.sum(expo_terms, axis=2, keepdims=True)
    token_max = (top_logit[..., 0] + jnp.log(total[..., 0])) / SHARPNESS
    return (token_max, expo_terms / total)


def merge_halves(first, second):
    teach_top = jnp.maximum(first[0], second[0])
    scale_one = jnp.exp(first[0] - teach_top)
    scale_two = jnp.exp(second[0] - teach_top)
    stud_top = jnp.maximum(first[3], second[3])
    fact_one = jnp.exp(first[3] - stud_top)
    fact_two = jnp.exp(second[3] - stud_top)
    return (
        teach_top,
        first[1] * scale_one + second[1] * scale_two,
        first[2] * scale_one + second[2] * scale_two,
        stud_top,
        first[4] * fact_one + second[4] * fact_two,
    )


def pair_sum(value):
    return value + lax.ppermute(value, "section", [(0, 1), (1, 0)])


def spread_sum(value, axis, size):
    pieces = value.reshape(size, -1, value.shape[-1])
    summed = lax.all_to_all(pieces, axis, 0, 0, tiled=True).sum(axis=0)
    spread = jnp.broadcast_to(summed[None], pieces.shape)
    return lax.all_to_all(spread, axis, 0, 0, tiled=True).reshape(value.shape)


def split_three(value):
    high = lax.reduce_precision(value, exponent_bits=8, mantissa_bits=7)
    rest = value - high
    middle = lax.reduce_precision(rest, exponent_bits=8, mantissa_bits=7)
    return high, middle, rest - middle


def lane_row(width, entries):
    lane = jnp.arange(width)[None, :]
    row = jnp.zeros((entries[0].shape[0], width), jnp.float32)
    for place, entry in enumerate(entries):
        spots = entry.shape[1]
        for spot in range(spots):
            row = jnp.where(lane == place * spots + spot, entry[:, spot : spot + 1].astype(jnp.float32), row)
    return row.astype(jnp.bfloat16)[:, None, :]


def score_kernel(
    count_ref, order_ref, slot_ref, qlen_ref, len_ref, q_ref, p_ref, pt_ref, pulled_ref, stud_ref
):
    _, num_tokens, vec_dim = q_ref.shape
    pass_tokens = p_ref.shape[1]
    group = GROUP
    base = pl.program_id(0) * group

    @pl.when(base < count_ref[0])
    def _score():
        for spot in range(group):
            at = order_ref[base + spot]
            slot = slot_ref[at]
            limit = len_ref[slot]
            logits = (
                lax.dot_general(
                    p_ref[slot], q_ref[at], (((1,), (1,)), ((), ())), preferred_element_type=jnp.float32
                )
                * SHARPNESS
            )
            in_range = lax.broadcasted_iota(jnp.int32, (pass_tokens, num_tokens), 0) < limit
            logits = jnp.where(in_range, logits, NEGATIVE)
            top_logit = jnp.max(logits, axis=0, keepdims=True)
            expo_terms = jnp.where(in_range, jnp.exp(logits - top_logit), 0.0)
            total = jnp.sum(expo_terms, axis=0, keepdims=True)
            token_max = (top_logit + jnp.log(total)) / SHARPNESS
            weight = (expo_terms / total).astype(jnp.bfloat16)
            pulled = jnp.dot(pt_ref[slot], weight, preferred_element_type=jnp.float32)
            pulled_ref[at] = pulled.T.astype(jnp.bfloat16)
            cols = lax.broadcasted_iota(jnp.int32, (1, num_tokens), 1)
            score = jnp.sum(jnp.where(cols < qlen_ref[at], token_max, 0.0))
            stud_ref[pl.ds(at, 1), :] = jnp.full((1, stud_ref.shape[1]), score, jnp.float32)

    @pl.when(base >= count_ref[0])
    def _empty():
        for spot in range(group):
            at = order_ref[base + spot]
            pulled_ref[at] = jnp.zeros((num_tokens, vec_dim), jnp.bfloat16)
            stud_ref[pl.ds(at, 1), :] = jnp.zeros((1, stud_ref.shape[1]), jnp.float32)


def owner_scores(q_rows, passages, slot_at, qlen_at, pass_len):
    slots, num_tokens, vec_dim = q_rows.shape
    held, pass_tokens, _ = passages.shape
    used = qlen_at > 0
    count = jnp.sum(used.astype(jnp.int32))
    place = jnp.where(
        used, jnp.cumsum(used) - 1, count + jnp.cumsum(jnp.logical_not(used)) - 1
    ).astype(jnp.int32)
    order = jnp.sum(
        jnp.where(place[None, :] == jnp.arange(slots)[:, None], jnp.arange(slots)[None, :], 0), axis=1
    ).astype(jnp.int32)
    whole = lambda i, *_: (0, 0, 0)
    grid_spec = pltpu.PrefetchScalarGridSpec(
        num_scalar_prefetch=5,
        grid=(slots // GROUP,),
        in_specs=[
            pl.BlockSpec((slots, num_tokens, vec_dim), whole),
            pl.BlockSpec((held, pass_tokens, vec_dim), whole),
            pl.BlockSpec((held, vec_dim, pass_tokens), whole),
        ],
        out_specs=[
            pl.BlockSpec((slots, num_tokens, vec_dim), whole),
            pl.BlockSpec((slots, 128), lambda i, *_: (0, 0)),
        ],
    )
    flops = 4 * slots * num_tokens * pass_tokens * vec_dim
    moved = 2 * (2 * held * pass_tokens * vec_dim + 2 * slots * num_tokens * vec_dim)
    return pl.pallas_call(
        score_kernel,
        grid_spec=grid_spec,
        out_shape=[
            jax.ShapeDtypeStruct((slots, num_tokens, vec_dim), jnp.bfloat16),
            jax.ShapeDtypeStruct((slots, 128), jnp.float32),
        ],
        compiler_params=pltpu.CompilerParams(vmem_limit_bytes=60 * 1024 * 1024),
        cost_estimate=pl.CostEstimate(
            flops=flops, transcendentals=slots * num_tokens * pass_tokens, bytes_accessed=moved
        ),
    )(
        count.reshape(1),
        order,
        slot_at,
        qlen_at,
        pass_len,
        q_rows,
        passages,
        jnp.swapaxes(passages, 1, 2),
    )


def local(hidden, proj, passages, pass_len, query_len, cand_owner, cand_slot, teacher):
    num_queries, num_tokens, feat_half = hidden.shape
    vec_dim = proj.shape[1]
    held = passages.shape[0]
    owners = lax.axis_size("shard")
    flat_h = hidden.reshape(num_queries * num_tokens, feat_half)
    partial_in = jnp.dot(flat_h, proj, preferred_element_type=jnp.float32).reshape(
        num_queries, num_tokens, vec_dim
    )
    proj_in = pair_sum(partial_in)
    inv_norm = lax.rsqrt(jnp.sum(proj_in * proj_in, axis=2, keepdims=True) + EPSILON)
    query_vecs = (proj_in * inv_norm).astype(jnp.bfloat16)
    tok_mask = jnp.arange(num_tokens)[None, :] < query_len[:, None]
    owner_ids = cand_owner.reshape(-1)
    slot_ids = cand_slot.reshape(-1)
    requests = owner_ids.shape[0]
    cand_half = requests // num_queries
    capacity = CAPACITY
    slots = owners * capacity
    onehot = (owner_ids[:, None] == jnp.arange(owners)[None, :]).astype(jnp.int32)
    rank_ids = jnp.sum((jnp.cumsum(onehot, axis=0) - onehot) * onehot, axis=1)
    buf_pos = owner_ids * capacity + rank_ids
    query_of = jnp.arange(requests) // cand_half
    pick = buf_pos[None, :] == jnp.arange(slots)[:, None]
    slot_query = jnp.any(pick[:, :, None] & (query_of[:, None] == jnp.arange(num_queries))[None], axis=1)
    q_send = jnp.einsum(
        "sq,qid->sid", slot_query.astype(jnp.bfloat16), query_vecs, preferred_element_type=jnp.float32
    ).astype(jnp.bfloat16)
    slot_meta = jnp.sum(jnp.where(pick, slot_ids[None, :], 0), axis=1).reshape(owners, capacity)
    qlen_meta = jnp.sum(jnp.where(pick, query_len[query_of][None, :], 0), axis=1).reshape(owners, capacity)
    body = capacity * num_tokens
    payload = jnp.concatenate(
        [q_send.reshape(owners, body, vec_dim), lane_row(vec_dim, (slot_meta, qlen_meta))], axis=1
    )
    recv = lax.all_to_all(payload, "shard", 0, 0, tiled=True)
    q_rows = recv[:, :body, :].reshape(slots, num_tokens, vec_dim)
    slot_at = recv[:, body, :capacity].astype(jnp.int32).reshape(slots)
    qlen_at = recv[:, body, capacity : 2 * capacity].astype(jnp.int32).reshape(slots)
    pulled, stud_rows = owner_scores(q_rows, passages, slot_at, qlen_at, pass_len)
    stud_at = stud_rows[:, 0]
    pieces = tuple(piece.reshape(owners, capacity) for piece in split_three(stud_at))
    back = jnp.concatenate(
        [pulled.reshape(owners, body, vec_dim), lane_row(vec_dim, pieces)], axis=1
    )
    got = lax.all_to_all(back, "shard", 0, 0, tiled=True)
    got_pulled = got[:, :body, :].reshape(slots, num_tokens, vec_dim)
    take = pick.T.astype(jnp.bfloat16)
    mine = jnp.einsum("rs,sid->rid", take, got_pulled, preferred_element_type=jnp.float32)
    got_meta = got[:, body, : 3 * capacity].astype(jnp.float32).reshape(owners, 3, capacity)
    got_meta = jnp.transpose(got_meta, (1, 0, 2)).reshape(3, slots)
    parts = jnp.sum(jnp.where(pick[None], got_meta[:, :, None], 0.0), axis=1)
    student = ((parts[0] + parts[1]) + parts[2]).reshape(num_queries, cand_half)
    pulled_mine = mine.reshape(num_queries, cand_half, num_tokens, vec_dim)
    teach_top = jnp.max(teacher, axis=1)
    teach_exp = jnp.exp(teacher - teach_top[:, None])
    teach_sum = jnp.sum(teach_exp, axis=1)
    teach_wsum = jnp.sum(teach_exp * (teacher - student), axis=1)
    stud_top = jnp.max(student, axis=1)
    stud_sum = jnp.sum(jnp.exp(student - stud_top[:, None]), axis=1)
    top_teach, sum_teach, wsum_teach, top_stud, sum_stud = combined_all(
        (teach_top, teach_sum, teach_wsum, stud_top, stud_sum), "section", merge_halves
    )
    lse_teach = top_teach + jnp.log(sum_teach)
    lse_stud = top_stud + jnp.log(sum_stud)
    kl_div = wsum_teach / sum_teach - lse_teach + lse_stud
    score_grad = jnp.exp(student - lse_stud[:, None]) - jnp.exp(teacher - lse_teach[:, None])
    half_grad = jnp.sum(score_grad[:, :, None, None] * pulled_mine, axis=1)
    half_grad = jnp.where(tok_mask[:, :, None], half_grad, 0.0)
    vec_grad = pair_sum(half_grad)
    cubed = inv_norm * inv_norm * inv_norm
    in_grad = inv_norm * vec_grad - cubed * proj_in * jnp.sum(
        proj_in * vec_grad, axis=2, keepdims=True
    )
    flat_in = in_grad.astype(jnp.bfloat16).reshape(num_queries * num_tokens, vec_dim)
    grad_hidden = jnp.dot(flat_in, proj.T, preferred_element_type=jnp.float32).astype(jnp.bfloat16)
    grad_hidden = grad_hidden.reshape(num_queries, num_tokens, feat_half)
    local_proj = jnp.dot(flat_h.T, flat_in, preferred_element_type=jnp.float32)
    grad_proj = spread_sum(local_proj, "shard", owners)
    return (kl_div, grad_hidden, grad_proj)


def solution(mesh):
    in_specs = (
        P("shard", None, "section"),
        P("section", None),
        P("shard", None, None),
        P("shard"),
        P("shard"),
        P("section", "shard", None, None),
        P("section", "shard", None),
        P("shard", "section"),
    )
    out_specs = (P("shard"), P("shard", None, "section"), P("section", None))
    return jax.shard_map(local, mesh=mesh, in_specs=in_specs, out_specs=out_specs, check_vma=False)
```

```python
import jax
import jax.numpy as jnp
from jax import lax
from jax.sharding import PartitionSpec as P
from jax.experimental import pallas as pl
from jax.experimental.pallas import tpu as pltpu

SHARPNESS = 64.0
EPSILON = 1e-06
NEGATIVE = -1e30
CAPACITY = 2
GROUP = 16


def combined_all(value, axis, join):
    pieces = jax.tree.map(lambda part: lax.all_gather(part, axis), value)
    head = jax.tree.map(lambda part: part[0], pieces)
    tail = jax.tree.map(lambda part: part[1:], pieces)
    running, _ = lax.scan(lambda running, section: (join(running, section), None), head, tail)
    return running


def token_scores(q_rows, blocks, cand_lens):
    logits = (
        jnp.einsum("bid,btd->bit", q_rows, blocks, preferred_element_type=jnp.float32) * SHARPNESS
    )
    in_range = jnp.arange(blocks.shape[1])[None, None, :] < cand_lens[:, None, None]
    logits = jnp.where(in_range, logits, NEGATIVE)
    top_logit = jnp.max(logits, axis=2, keepdims=True)
    expo_terms = jnp.where(in_range, jnp.exp(logits - top_logit), 0.0)
    total = jnp.sum(expo_terms, axis=2, keepdims=True)
    token_max = (top_logit[..., 0] + jnp.log(total[..., 0])) / SHARPNESS
    return (token_max, expo_terms / total)


def merge_halves(first, second):
    teach_top = jnp.maximum(first[0], second[0])
    scale_one = jnp.exp(first[0] - teach_top)
    scale_two = jnp.exp(second[0] - teach_top)
    stud_top = jnp.maximum(first[3], second[3])
    fact_one = jnp.exp(first[3] - stud_top)
    fact_two = jnp.exp(second[3] - stud_top)
    return (
        teach_top,
        first[1] * scale_one + second[1] * scale_two,
        first[2] * scale_one + second[2] * scale_two,
        stud_top,
        first[4] * fact_one + second[4] * fact_two,
    )


def pair_sum(value):
    return value + lax.ppermute(value, "section", [(0, 1), (1, 0)])


def spread_sum(value, axis, size):
    pieces = value.reshape(size, -1, value.shape[-1])
    summed = lax.all_to_all(pieces, axis, 0, 0, tiled=True).sum(axis=0)
    spread = jnp.broadcast_to(summed[None], pieces.shape)
    return lax.all_to_all(spread, axis, 0, 0, tiled=True).reshape(value.shape)


def split_three(value):
    high = lax.reduce_precision(value, exponent_bits=8, mantissa_bits=7)
    rest = value - high
    middle = lax.reduce_precision(rest, exponent_bits=8, mantissa_bits=7)
    return high, middle, rest - middle


def lane_row(width, entries):
    lane = jnp.arange(width)[None, :]
    row = jnp.zeros((entries[0].shape[0], width), jnp.float32)
    for place, entry in enumerate(entries):
        spots = entry.shape[1]
        for spot in range(spots):
            row = jnp.where(lane == place * spots + spot, entry[:, spot : spot + 1].astype(jnp.float32), row)
    return row.astype(jnp.bfloat16)[:, None, :]


def score_kernel(slot_ref, qlen_ref, len_ref, q_ref, p_ref, pt_ref, pulled_ref, stud_ref):
    group, num_tokens, _ = q_ref.shape
    pass_tokens = p_ref.shape[1]
    base = pl.program_id(0) * group
    for spot in range(group):
        slot = slot_ref[base + spot]
        limit = len_ref[slot]
        logits = (
            lax.dot_general(
                p_ref[slot], q_ref[spot], (((1,), (1,)), ((), ())), preferred_element_type=jnp.float32
            )
            * SHARPNESS
        )
        in_range = lax.broadcasted_iota(jnp.int32, (pass_tokens, num_tokens), 0) < limit
        logits = jnp.where(in_range, logits, NEGATIVE)
        top_logit = jnp.max(logits, axis=0, keepdims=True)
        expo_terms = jnp.where(in_range, jnp.exp(logits - top_logit), 0.0)
        total = jnp.sum(expo_terms, axis=0, keepdims=True)
        token_max = (top_logit + jnp.log(total)) / SHARPNESS
        weight = (expo_terms / total).astype(jnp.bfloat16)
        pulled = jnp.dot(pt_ref[slot], weight, preferred_element_type=jnp.float32)
        pulled_ref[spot] = pulled.T.astype(jnp.bfloat16)
        cols = lax.broadcasted_iota(jnp.int32, (1, num_tokens), 1)
        score = jnp.sum(jnp.where(cols < qlen_ref[base + spot], token_max, 0.0))
        stud_ref[pl.ds(spot, 1), :] = jnp.full((1, stud_ref.shape[1]), score, jnp.float32)


def owner_scores(q_rows, passages, slot_at, qlen_at, pass_len):
    slots, num_tokens, vec_dim = q_rows.shape
    held, pass_tokens, _ = passages.shape
    group = GROUP
    grid_spec = pltpu.PrefetchScalarGridSpec(
        num_scalar_prefetch=3,
        grid=(slots // group,),
        in_specs=[
            pl.BlockSpec((group, num_tokens, vec_dim), lambda i, *_: (i, 0, 0)),
            pl.BlockSpec((held, pass_tokens, vec_dim), lambda i, *_: (0, 0, 0)),
            pl.BlockSpec((held, vec_dim, pass_tokens), lambda i, *_: (0, 0, 0)),
        ],
        out_specs=[
            pl.BlockSpec((group, num_tokens, vec_dim), lambda i, *_: (i, 0, 0)),
            pl.BlockSpec((group, 128), lambda i, *_: (i, 0)),
        ],
    )
    flops = 4 * slots * num_tokens * pass_tokens * vec_dim
    moved = 2 * (2 * held * pass_tokens * vec_dim + 2 * slots * num_tokens * vec_dim)
    return pl.pallas_call(
        score_kernel,
        grid_spec=grid_spec,
        out_shape=[
            jax.ShapeDtypeStruct((slots, num_tokens, vec_dim), jnp.bfloat16),
            jax.ShapeDtypeStruct((slots, 128), jnp.float32),
        ],
        compiler_params=pltpu.CompilerParams(vmem_limit_bytes=60 * 1024 * 1024),
        cost_estimate=pl.CostEstimate(
            flops=flops, transcendentals=slots * num_tokens * pass_tokens, bytes_accessed=moved
        ),
    )(slot_at, qlen_at, pass_len, q_rows, passages, jnp.swapaxes(passages, 1, 2))


def local(hidden, proj, passages, pass_len, query_len, cand_owner, cand_slot, teacher):
    num_queries, num_tokens, feat_half = hidden.shape
    vec_dim = proj.shape[1]
    held = passages.shape[0]
    owners = lax.axis_size("shard")
    flat_h = hidden.reshape(num_queries * num_tokens, feat_half)
    partial_in = jnp.dot(flat_h, proj, preferred_element_type=jnp.float32).reshape(
        num_queries, num_tokens, vec_dim
    )
    proj_in = pair_sum(partial_in)
    inv_norm = lax.rsqrt(jnp.sum(proj_in * proj_in, axis=2, keepdims=True) + EPSILON)
    query_vecs = (proj_in * inv_norm).astype(jnp.bfloat16)
    tok_mask = jnp.arange(num_tokens)[None, :] < query_len[:, None]
    owner_ids = cand_owner.reshape(-1)
    slot_ids = cand_slot.reshape(-1)
    requests = owner_ids.shape[0]
    cand_half = requests // num_queries
    capacity = CAPACITY
    slots = owners * capacity
    onehot = (owner_ids[:, None] == jnp.arange(owners)[None, :]).astype(jnp.int32)
    rank_ids = jnp.sum((jnp.cumsum(onehot, axis=0) - onehot) * onehot, axis=1)
    buf_pos = owner_ids * capacity + rank_ids
    query_of = jnp.arange(requests) // cand_half
    pick = buf_pos[None, :] == jnp.arange(slots)[:, None]
    slot_query = jnp.any(pick[:, :, None] & (query_of[:, None] == jnp.arange(num_queries))[None], axis=1)
    q_send = jnp.einsum(
        "sq,qid->sid", slot_query.astype(jnp.bfloat16), query_vecs, preferred_element_type=jnp.float32
    ).astype(jnp.bfloat16)
    slot_meta = jnp.sum(jnp.where(pick, slot_ids[None, :], 0), axis=1).reshape(owners, capacity)
    qlen_meta = jnp.sum(jnp.where(pick, query_len[query_of][None, :], 0), axis=1).reshape(owners, capacity)
    body = capacity * num_tokens
    payload = jnp.concatenate(
        [q_send.reshape(owners, body, vec_dim), lane_row(vec_dim, (slot_meta, qlen_meta))], axis=1
    )
    recv = lax.all_to_all(payload, "shard", 0, 0, tiled=True)
    q_rows = recv[:, :body, :].reshape(slots, num_tokens, vec_dim)
    slot_at = recv[:, body, :capacity].astype(jnp.int32).reshape(slots)
    qlen_at = recv[:, body, capacity : 2 * capacity].astype(jnp.int32).reshape(slots)
    pulled, stud_rows = owner_scores(q_rows, passages, slot_at, qlen_at, pass_len)
    stud_at = stud_rows[:, 0]
    pieces = tuple(piece.reshape(owners, capacity) for piece in split_three(stud_at))
    back = jnp.concatenate(
        [pulled.reshape(owners, body, vec_dim), lane_row(vec_dim, pieces)], axis=1
    )
    got = lax.all_to_all(back, "shard", 0, 0, tiled=True)
    got_pulled = got[:, :body, :].reshape(slots, num_tokens, vec_dim)
    take = pick.T.astype(jnp.bfloat16)
    mine = jnp.einsum("rs,sid->rid", take, got_pulled, preferred_element_type=jnp.float32)
    got_meta = got[:, body, : 3 * capacity].astype(jnp.float32).reshape(owners, 3, capacity)
    got_meta = jnp.transpose(got_meta, (1, 0, 2)).reshape(3, slots)
    parts = jnp.sum(jnp.where(pick[None], got_meta[:, :, None], 0.0), axis=1)
    student = ((parts[0] + parts[1]) + parts[2]).reshape(num_queries, cand_half)
    pulled_mine = mine.reshape(num_queries, cand_half, num_tokens, vec_dim)
    teach_top = jnp.max(teacher, axis=1)
    teach_exp = jnp.exp(teacher - teach_top[:, None])
    teach_sum = jnp.sum(teach_exp, axis=1)
    teach_wsum = jnp.sum(teach_exp * (teacher - student), axis=1)
    stud_top = jnp.max(student, axis=1)
    stud_sum = jnp.sum(jnp.exp(student - stud_top[:, None]), axis=1)
    top_teach, sum_teach, wsum_teach, top_stud, sum_stud = combined_all(
        (teach_top, teach_sum, teach_wsum, stud_top, stud_sum), "section", merge_halves
    )
    lse_teach = top_teach + jnp.log(sum_teach)
    lse_stud = top_stud + jnp.log(sum_stud)
    kl_div = wsum_teach / sum_teach - lse_teach + lse_stud
    score_grad = jnp.exp(student - lse_stud[:, None]) - jnp.exp(teacher - lse_teach[:, None])
    half_grad = jnp.sum(score_grad[:, :, None, None] * pulled_mine, axis=1)
    half_grad = jnp.where(tok_mask[:, :, None], half_grad, 0.0)
    vec_grad = pair_sum(half_grad)
    cubed = inv_norm * inv_norm * inv_norm
    in_grad = inv_norm * vec_grad - cubed * proj_in * jnp.sum(
        proj_in * vec_grad, axis=2, keepdims=True
    )
    flat_in = in_grad.astype(jnp.bfloat16).reshape(num_queries * num_tokens, vec_dim)
    grad_hidden = jnp.dot(flat_in, proj.T, preferred_element_type=jnp.float32).astype(jnp.bfloat16)
    grad_hidden = grad_hidden.reshape(num_queries, num_tokens, feat_half)
    local_proj = jnp.dot(flat_h.T, flat_in, preferred_element_type=jnp.float32)
    grad_proj = spread_sum(local_proj, "shard", owners)
    return (kl_div, grad_hidden, grad_proj)


def solution(mesh):
    in_specs = (
        P("shard", None, "section"),
        P("section", None),
        P("shard", None, None),
        P("shard"),
        P("shard"),
        P("section", "shard", None, None),
        P("section", "shard", None),
        P("shard", "section"),
    )
    out_specs = (P("shard"), P("shard", None, "section"), P("section", None))
    return jax.shard_map(local, mesh=mesh, in_specs=in_specs, out_specs=out_specs, check_vma=False)
```

```python
import jax
import jax.numpy as jnp
from jax import lax
from jax.sharding import PartitionSpec as P
from jax.experimental import pallas as pl
from jax.experimental.pallas import tpu as pltpu

SHARPNESS = 64.0
EPSILON = 1e-06
NEGATIVE = -1e30
CAPACITY = 2
GROUP = 32


def combined_all(value, axis, join):
    pieces = jax.tree.map(lambda part: lax.all_gather(part, axis), value)
    head = jax.tree.map(lambda part: part[0], pieces)
    tail = jax.tree.map(lambda part: part[1:], pieces)
    running, _ = lax.scan(lambda running, section: (join(running, section), None), head, tail)
    return running


def token_scores(q_rows, blocks, cand_lens):
    logits = (
        jnp.einsum("bid,btd->bit", q_rows, blocks, preferred_element_type=jnp.float32) * SHARPNESS
    )
    in_range = jnp.arange(blocks.shape[1])[None, None, :] < cand_lens[:, None, None]
    logits = jnp.where(in_range, logits, NEGATIVE)
    top_logit = jnp.max(logits, axis=2, keepdims=True)
    expo_terms = jnp.where(in_range, jnp.exp(logits - top_logit), 0.0)
    total = jnp.sum(expo_terms, axis=2, keepdims=True)
    token_max = (top_logit[..., 0] + jnp.log(total[..., 0])) / SHARPNESS
    return (token_max, expo_terms / total)


def merge_halves(first, second):
    teach_top = jnp.maximum(first[0], second[0])
    scale_one = jnp.exp(first[0] - teach_top)
    scale_two = jnp.exp(second[0] - teach_top)
    stud_top = jnp.maximum(first[3], second[3])
    fact_one = jnp.exp(first[3] - stud_top)
    fact_two = jnp.exp(second[3] - stud_top)
    return (
        teach_top,
        first[1] * scale_one + second[1] * scale_two,
        first[2] * scale_one + second[2] * scale_two,
        stud_top,
        first[4] * fact_one + second[4] * fact_two,
    )


def pair_sum(value):
    return value + lax.ppermute(value, "section", [(0, 1), (1, 0)])


def spread_sum(value, axis, size):
    pieces = value.reshape(size, -1, value.shape[-1])
    summed = lax.all_to_all(pieces, axis, 0, 0, tiled=True).sum(axis=0)
    spread = jnp.broadcast_to(summed[None], pieces.shape)
    return lax.all_to_all(spread, axis, 0, 0, tiled=True).reshape(value.shape)


def split_three(value):
    high = lax.reduce_precision(value, exponent_bits=8, mantissa_bits=7)
    rest = value - high
    middle = lax.reduce_precision(rest, exponent_bits=8, mantissa_bits=7)
    return high, middle, rest - middle


def lane_row(width, entries):
    lane = jnp.arange(width)[None, :]
    row = jnp.zeros((entries[0].shape[0], width), jnp.float32)
    for place, entry in enumerate(entries):
        spots = entry.shape[1]
        for spot in range(spots):
            row = jnp.where(lane == place * spots + spot, entry[:, spot : spot + 1].astype(jnp.float32), row)
    return row.astype(jnp.bfloat16)[:, None, :]


def score_kernel(slot_ref, qlen_ref, len_ref, q_ref, p_ref, pt_ref, pulled_ref, stud_ref):
    group, num_tokens, _ = q_ref.shape
    pass_tokens = p_ref.shape[1]
    base = pl.program_id(0) * group
    for spot in range(group):
        slot = slot_ref[base + spot]
        limit = len_ref[slot]
        logits = (
            lax.dot_general(
                p_ref[slot], q_ref[spot], (((1,), (1,)), ((), ())), preferred_element_type=jnp.float32
            )
            * SHARPNESS
        )
        in_range = lax.broadcasted_iota(jnp.int32, (pass_tokens, num_tokens), 0) < limit
        logits = jnp.where(in_range, logits, NEGATIVE)
        top_logit = jnp.max(logits, axis=0, keepdims=True)
        expo_terms = jnp.where(in_range, jnp.exp(logits - top_logit), 0.0)
        total = jnp.sum(expo_terms, axis=0, keepdims=True)
        token_max = (top_logit + jnp.log(total)) / SHARPNESS
        weight = (expo_terms / total).astype(jnp.bfloat16)
        pulled = jnp.dot(pt_ref[slot], weight, preferred_element_type=jnp.float32)
        pulled_ref[spot] = pulled.T.astype(jnp.bfloat16)
        cols = lax.broadcasted_iota(jnp.int32, (1, num_tokens), 1)
        score = jnp.sum(jnp.where(cols < qlen_ref[base + spot], token_max, 0.0))
        stud_ref[pl.ds(spot, 1), :] = jnp.full((1, stud_ref.shape[1]), score, jnp.float32)


def owner_scores(q_rows, passages, slot_at, qlen_at, pass_len):
    slots, num_tokens, vec_dim = q_rows.shape
    held, pass_tokens, _ = passages.shape
    group = GROUP
    grid_spec = pltpu.PrefetchScalarGridSpec(
        num_scalar_prefetch=3,
        grid=(slots // group,),
        in_specs=[
            pl.BlockSpec((group, num_tokens, vec_dim), lambda i, *_: (i, 0, 0)),
            pl.BlockSpec((held, pass_tokens, vec_dim), lambda i, *_: (0, 0, 0)),
            pl.BlockSpec((held, vec_dim, pass_tokens), lambda i, *_: (0, 0, 0)),
        ],
        out_specs=[
            pl.BlockSpec((group, num_tokens, vec_dim), lambda i, *_: (i, 0, 0)),
            pl.BlockSpec((group, 128), lambda i, *_: (i, 0)),
        ],
    )
    flops = 4 * slots * num_tokens * pass_tokens * vec_dim
    moved = 2 * (2 * held * pass_tokens * vec_dim + 2 * slots * num_tokens * vec_dim)
    return pl.pallas_call(
        score_kernel,
        grid_spec=grid_spec,
        out_shape=[
            jax.ShapeDtypeStruct((slots, num_tokens, vec_dim), jnp.bfloat16),
            jax.ShapeDtypeStruct((slots, 128), jnp.float32),
        ],
        compiler_params=pltpu.CompilerParams(vmem_limit_bytes=60 * 1024 * 1024),
        cost_estimate=pl.CostEstimate(
            flops=flops, transcendentals=slots * num_tokens * pass_tokens, bytes_accessed=moved
        ),
    )(slot_at, qlen_at, pass_len, q_rows, passages, jnp.swapaxes(passages, 1, 2))


def local(hidden, proj, passages, pass_len, query_len, cand_owner, cand_slot, teacher):
    num_queries, num_tokens, feat_half = hidden.shape
    vec_dim = proj.shape[1]
    held = passages.shape[0]
    owners = lax.axis_size("shard")
    flat_h = hidden.reshape(num_queries * num_tokens, feat_half)
    partial_in = jnp.dot(flat_h, proj, preferred_element_type=jnp.float32).reshape(
        num_queries, num_tokens, vec_dim
    )
    proj_in = pair_sum(partial_in)
    inv_norm = lax.rsqrt(jnp.sum(proj_in * proj_in, axis=2, keepdims=True) + EPSILON)
    query_vecs = (proj_in * inv_norm).astype(jnp.bfloat16)
    tok_mask = jnp.arange(num_tokens)[None, :] < query_len[:, None]
    owner_ids = cand_owner.reshape(-1)
    slot_ids = cand_slot.reshape(-1)
    requests = owner_ids.shape[0]
    cand_half = requests // num_queries
    capacity = CAPACITY
    slots = owners * capacity
    onehot = (owner_ids[:, None] == jnp.arange(owners)[None, :]).astype(jnp.int32)
    rank_ids = jnp.sum((jnp.cumsum(onehot, axis=0) - onehot) * onehot, axis=1)
    buf_pos = owner_ids * capacity + rank_ids
    query_of = jnp.arange(requests) // cand_half
    pick = buf_pos[None, :] == jnp.arange(slots)[:, None]
    slot_query = jnp.any(pick[:, :, None] & (query_of[:, None] == jnp.arange(num_queries))[None], axis=1)
    q_send = jnp.einsum(
        "sq,qid->sid", slot_query.astype(jnp.bfloat16), query_vecs, preferred_element_type=jnp.float32
    ).astype(jnp.bfloat16)
    slot_meta = jnp.sum(jnp.where(pick, slot_ids[None, :], 0), axis=1).reshape(owners, capacity)
    qlen_meta = jnp.sum(jnp.where(pick, query_len[query_of][None, :], 0), axis=1).reshape(owners, capacity)
    body = capacity * num_tokens
    payload = jnp.concatenate(
        [q_send.reshape(owners, body, vec_dim), lane_row(vec_dim, (slot_meta, qlen_meta))], axis=1
    )
    recv = lax.all_to_all(payload, "shard", 0, 0, tiled=True)
    q_rows = recv[:, :body, :].reshape(slots, num_tokens, vec_dim)
    slot_at = recv[:, body, :capacity].astype(jnp.int32).reshape(slots)
    qlen_at = recv[:, body, capacity : 2 * capacity].astype(jnp.int32).reshape(slots)
    pulled, stud_rows = owner_scores(q_rows, passages, slot_at, qlen_at, pass_len)
    stud_at = stud_rows[:, 0]
    pieces = tuple(piece.reshape(owners, capacity) for piece in split_three(stud_at))
    back = jnp.concatenate(
        [pulled.reshape(owners, body, vec_dim), lane_row(vec_dim, pieces)], axis=1
    )
    got = lax.all_to_all(back, "shard", 0, 0, tiled=True)
    got_pulled = got[:, :body, :].reshape(slots, num_tokens, vec_dim)
    take = pick.T.astype(jnp.bfloat16)
    mine = jnp.einsum("rs,sid->rid", take, got_pulled, preferred_element_type=jnp.float32)
    got_meta = got[:, body, : 3 * capacity].astype(jnp.float32).reshape(owners, 3, capacity)
    got_meta = jnp.transpose(got_meta, (1, 0, 2)).reshape(3, slots)
    parts = jnp.sum(jnp.where(pick[None], got_meta[:, :, None], 0.0), axis=1)
    student = ((parts[0] + parts[1]) + parts[2]).reshape(num_queries, cand_half)
    pulled_mine = mine.reshape(num_queries, cand_half, num_tokens, vec_dim)
    teach_top = jnp.max(teacher, axis=1)
    teach_exp = jnp.exp(teacher - teach_top[:, None])
    teach_sum = jnp.sum(teach_exp, axis=1)
    teach_wsum = jnp.sum(teach_exp * (teacher - student), axis=1)
    stud_top = jnp.max(student, axis=1)
    stud_sum = jnp.sum(jnp.exp(student - stud_top[:, None]), axis=1)
    top_teach, sum_teach, wsum_teach, top_stud, sum_stud = combined_all(
        (teach_top, teach_sum, teach_wsum, stud_top, stud_sum), "section", merge_halves
    )
    lse_teach = top_teach + jnp.log(sum_teach)
    lse_stud = top_stud + jnp.log(sum_stud)
    kl_div = wsum_teach / sum_teach - lse_teach + lse_stud
    score_grad = jnp.exp(student - lse_stud[:, None]) - jnp.exp(teacher - lse_teach[:, None])
    half_grad = jnp.sum(score_grad[:, :, None, None] * pulled_mine, axis=1)
    half_grad = jnp.where(tok_mask[:, :, None], half_grad, 0.0)
    vec_grad = pair_sum(half_grad)
    cubed = inv_norm * inv_norm * inv_norm
    in_grad = inv_norm * vec_grad - cubed * proj_in * jnp.sum(
        proj_in * vec_grad, axis=2, keepdims=True
    )
    flat_in = in_grad.astype(jnp.bfloat16).reshape(num_queries * num_tokens, vec_dim)
    grad_hidden = jnp.dot(flat_in, proj.T, preferred_element_type=jnp.float32).astype(jnp.bfloat16)
    grad_hidden = grad_hidden.reshape(num_queries, num_tokens, feat_half)
    local_proj = jnp.dot(flat_h.T, flat_in, preferred_element_type=jnp.float32)
    grad_proj = spread_sum(local_proj, "shard", owners)
    return (kl_div, grad_hidden, grad_proj)


def solution(mesh):
    in_specs = (
        P("shard", None, "section"),
        P("section", None),
        P("shard", None, None),
        P("shard"),
        P("shard"),
        P("section", "shard", None, None),
        P("section", "shard", None),
        P("shard", "section"),
    )
    out_specs = (P("shard"), P("shard", None, "section"), P("section", None))
    return jax.shard_map(local, mesh=mesh, in_specs=in_specs, out_specs=out_specs, check_vma=False)
```

```python
import jax
import jax.numpy as jnp
from jax import lax
from jax.sharding import PartitionSpec as P
from jax.experimental import pallas as pl
from jax.experimental.pallas import tpu as pltpu

SHARPNESS = 64.0
EPSILON = 1e-06
NEGATIVE = -1e30
CAPACITY = 2
GROUP = 64


def combined_all(value, axis, join):
    pieces = jax.tree.map(lambda part: lax.all_gather(part, axis), value)
    head = jax.tree.map(lambda part: part[0], pieces)
    tail = jax.tree.map(lambda part: part[1:], pieces)
    running, _ = lax.scan(lambda running, section: (join(running, section), None), head, tail)
    return running


def token_scores(q_rows, blocks, cand_lens):
    logits = (
        jnp.einsum("bid,btd->bit", q_rows, blocks, preferred_element_type=jnp.float32) * SHARPNESS
    )
    in_range = jnp.arange(blocks.shape[1])[None, None, :] < cand_lens[:, None, None]
    logits = jnp.where(in_range, logits, NEGATIVE)
    top_logit = jnp.max(logits, axis=2, keepdims=True)
    expo_terms = jnp.where(in_range, jnp.exp(logits - top_logit), 0.0)
    total = jnp.sum(expo_terms, axis=2, keepdims=True)
    token_max = (top_logit[..., 0] + jnp.log(total[..., 0])) / SHARPNESS
    return (token_max, expo_terms / total)


def merge_halves(first, second):
    teach_top = jnp.maximum(first[0], second[0])
    scale_one = jnp.exp(first[0] - teach_top)
    scale_two = jnp.exp(second[0] - teach_top)
    stud_top = jnp.maximum(first[3], second[3])
    fact_one = jnp.exp(first[3] - stud_top)
    fact_two = jnp.exp(second[3] - stud_top)
    return (
        teach_top,
        first[1] * scale_one + second[1] * scale_two,
        first[2] * scale_one + second[2] * scale_two,
        stud_top,
        first[4] * fact_one + second[4] * fact_two,
    )


def pair_sum(value):
    return value + lax.ppermute(value, "section", [(0, 1), (1, 0)])


def spread_sum(value, axis, size):
    pieces = value.reshape(size, -1, value.shape[-1])
    summed = lax.all_to_all(pieces, axis, 0, 0, tiled=True).sum(axis=0)
    spread = jnp.broadcast_to(summed[None], pieces.shape)
    return lax.all_to_all(spread, axis, 0, 0, tiled=True).reshape(value.shape)


def split_three(value):
    high = lax.reduce_precision(value, exponent_bits=8, mantissa_bits=7)
    rest = value - high
    middle = lax.reduce_precision(rest, exponent_bits=8, mantissa_bits=7)
    return high, middle, rest - middle


def lane_row(width, entries):
    lane = jnp.arange(width)[None, :]
    row = jnp.zeros((entries[0].shape[0], width), jnp.float32)
    for place, entry in enumerate(entries):
        spots = entry.shape[1]
        for spot in range(spots):
            row = jnp.where(lane == place * spots + spot, entry[:, spot : spot + 1].astype(jnp.float32), row)
    return row.astype(jnp.bfloat16)[:, None, :]


def score_kernel(slot_ref, qlen_ref, len_ref, q_ref, p_ref, pt_ref, pulled_ref, stud_ref):
    group, num_tokens, _ = q_ref.shape
    pass_tokens = p_ref.shape[1]
    base = pl.program_id(0) * group
    for spot in range(group):
        slot = slot_ref[base + spot]
        limit = len_ref[slot]
        logits = (
            lax.dot_general(
                p_ref[slot], q_ref[spot], (((1,), (1,)), ((), ())), preferred_element_type=jnp.float32
            )
            * SHARPNESS
        )
        in_range = lax.broadcasted_iota(jnp.int32, (pass_tokens, num_tokens), 0) < limit
        logits = jnp.where(in_range, logits, NEGATIVE)
        top_logit = jnp.max(logits, axis=0, keepdims=True)
        expo_terms = jnp.where(in_range, jnp.exp(logits - top_logit), 0.0)
        total = jnp.sum(expo_terms, axis=0, keepdims=True)
        token_max = (top_logit + jnp.log(total)) / SHARPNESS
        weight = (expo_terms / total).astype(jnp.bfloat16)
        pulled = jnp.dot(pt_ref[slot], weight, preferred_element_type=jnp.float32)
        pulled_ref[spot] = pulled.T.astype(jnp.bfloat16)
        cols = lax.broadcasted_iota(jnp.int32, (1, num_tokens), 1)
        score = jnp.sum(jnp.where(cols < qlen_ref[base + spot], token_max, 0.0))
        stud_ref[pl.ds(spot, 1), :] = jnp.full((1, stud_ref.shape[1]), score, jnp.float32)


def owner_scores(q_rows, passages, slot_at, qlen_at, pass_len):
    slots, num_tokens, vec_dim = q_rows.shape
    held, pass_tokens, _ = passages.shape
    group = GROUP
    grid_spec = pltpu.PrefetchScalarGridSpec(
        num_scalar_prefetch=3,
        grid=(slots // group,),
        in_specs=[
            pl.BlockSpec((group, num_tokens, vec_dim), lambda i, *_: (i, 0, 0)),
            pl.BlockSpec((held, pass_tokens, vec_dim), lambda i, *_: (0, 0, 0)),
            pl.BlockSpec((held, vec_dim, pass_tokens), lambda i, *_: (0, 0, 0)),
        ],
        out_specs=[
            pl.BlockSpec((group, num_tokens, vec_dim), lambda i, *_: (i, 0, 0)),
            pl.BlockSpec((group, 128), lambda i, *_: (i, 0)),
        ],
    )
    flops = 4 * slots * num_tokens * pass_tokens * vec_dim
    moved = 2 * (2 * held * pass_tokens * vec_dim + 2 * slots * num_tokens * vec_dim)
    return pl.pallas_call(
        score_kernel,
        grid_spec=grid_spec,
        out_shape=[
            jax.ShapeDtypeStruct((slots, num_tokens, vec_dim), jnp.bfloat16),
            jax.ShapeDtypeStruct((slots, 128), jnp.float32),
        ],
        compiler_params=pltpu.CompilerParams(vmem_limit_bytes=60 * 1024 * 1024),
        cost_estimate=pl.CostEstimate(
            flops=flops, transcendentals=slots * num_tokens * pass_tokens, bytes_accessed=moved
        ),
    )(slot_at, qlen_at, pass_len, q_rows, passages, jnp.swapaxes(passages, 1, 2))


def local(hidden, proj, passages, pass_len, query_len, cand_owner, cand_slot, teacher):
    num_queries, num_tokens, feat_half = hidden.shape
    vec_dim = proj.shape[1]
    held = passages.shape[0]
    owners = lax.axis_size("shard")
    flat_h = hidden.reshape(num_queries * num_tokens, feat_half)
    partial_in = jnp.dot(flat_h, proj, preferred_element_type=jnp.float32).reshape(
        num_queries, num_tokens, vec_dim
    )
    proj_in = pair_sum(partial_in)
    inv_norm = lax.rsqrt(jnp.sum(proj_in * proj_in, axis=2, keepdims=True) + EPSILON)
    query_vecs = (proj_in * inv_norm).astype(jnp.bfloat16)
    tok_mask = jnp.arange(num_tokens)[None, :] < query_len[:, None]
    owner_ids = cand_owner.reshape(-1)
    slot_ids = cand_slot.reshape(-1)
    requests = owner_ids.shape[0]
    cand_half = requests // num_queries
    capacity = CAPACITY
    slots = owners * capacity
    onehot = (owner_ids[:, None] == jnp.arange(owners)[None, :]).astype(jnp.int32)
    rank_ids = jnp.sum((jnp.cumsum(onehot, axis=0) - onehot) * onehot, axis=1)
    buf_pos = owner_ids * capacity + rank_ids
    query_of = jnp.arange(requests) // cand_half
    pick = buf_pos[None, :] == jnp.arange(slots)[:, None]
    slot_query = jnp.any(pick[:, :, None] & (query_of[:, None] == jnp.arange(num_queries))[None], axis=1)
    q_send = jnp.einsum(
        "sq,qid->sid", slot_query.astype(jnp.bfloat16), query_vecs, preferred_element_type=jnp.float32
    ).astype(jnp.bfloat16)
    slot_meta = jnp.sum(jnp.where(pick, slot_ids[None, :], 0), axis=1).reshape(owners, capacity)
    qlen_meta = jnp.sum(jnp.where(pick, query_len[query_of][None, :], 0), axis=1).reshape(owners, capacity)
    body = capacity * num_tokens
    payload = jnp.concatenate(
        [q_send.reshape(owners, body, vec_dim), lane_row(vec_dim, (slot_meta, qlen_meta))], axis=1
    )
    recv = lax.all_to_all(payload, "shard", 0, 0, tiled=True)
    q_rows = recv[:, :body, :].reshape(slots, num_tokens, vec_dim)
    slot_at = recv[:, body, :capacity].astype(jnp.int32).reshape(slots)
    qlen_at = recv[:, body, capacity : 2 * capacity].astype(jnp.int32).reshape(slots)
    pulled, stud_rows = owner_scores(q_rows, passages, slot_at, qlen_at, pass_len)
    stud_at = stud_rows[:, 0]
    pieces = tuple(piece.reshape(owners, capacity) for piece in split_three(stud_at))
    back = jnp.concatenate(
        [pulled.reshape(owners, body, vec_dim), lane_row(vec_dim, pieces)], axis=1
    )
    got = lax.all_to_all(back, "shard", 0, 0, tiled=True)
    got_pulled = got[:, :body, :].reshape(slots, num_tokens, vec_dim)
    take = pick.T.astype(jnp.bfloat16)
    mine = jnp.einsum("rs,sid->rid", take, got_pulled, preferred_element_type=jnp.float32)
    got_meta = got[:, body, : 3 * capacity].astype(jnp.float32).reshape(owners, 3, capacity)
    got_meta = jnp.transpose(got_meta, (1, 0, 2)).reshape(3, slots)
    parts = jnp.sum(jnp.where(pick[None], got_meta[:, :, None], 0.0), axis=1)
    student = ((parts[0] + parts[1]) + parts[2]).reshape(num_queries, cand_half)
    pulled_mine = mine.reshape(num_queries, cand_half, num_tokens, vec_dim)
    teach_top = jnp.max(teacher, axis=1)
    teach_exp = jnp.exp(teacher - teach_top[:, None])
    teach_sum = jnp.sum(teach_exp, axis=1)
    teach_wsum = jnp.sum(teach_exp * (teacher - student), axis=1)
    stud_top = jnp.max(student, axis=1)
    stud_sum = jnp.sum(jnp.exp(student - stud_top[:, None]), axis=1)
    top_teach, sum_teach, wsum_teach, top_stud, sum_stud = combined_all(
        (teach_top, teach_sum, teach_wsum, stud_top, stud_sum), "section", merge_halves
    )
    lse_teach = top_teach + jnp.log(sum_teach)
    lse_stud = top_stud + jnp.log(sum_stud)
    kl_div = wsum_teach / sum_teach - lse_teach + lse_stud
    score_grad = jnp.exp(student - lse_stud[:, None]) - jnp.exp(teacher - lse_teach[:, None])
    half_grad = jnp.sum(score_grad[:, :, None, None] * pulled_mine, axis=1)
    half_grad = jnp.where(tok_mask[:, :, None], half_grad, 0.0)
    vec_grad = pair_sum(half_grad)
    cubed = inv_norm * inv_norm * inv_norm
    in_grad = inv_norm * vec_grad - cubed * proj_in * jnp.sum(
        proj_in * vec_grad, axis=2, keepdims=True
    )
    flat_in = in_grad.astype(jnp.bfloat16).reshape(num_queries * num_tokens, vec_dim)
    grad_hidden = jnp.dot(flat_in, proj.T, preferred_element_type=jnp.float32).astype(jnp.bfloat16)
    grad_hidden = grad_hidden.reshape(num_queries, num_tokens, feat_half)
    local_proj = jnp.dot(flat_h.T, flat_in, preferred_element_type=jnp.float32)
    grad_proj = spread_sum(local_proj, "shard", owners)
    return (kl_div, grad_hidden, grad_proj)


def solution(mesh):
    in_specs = (
        P("shard", None, "section"),
        P("section", None),
        P("shard", None, None),
        P("shard"),
        P("shard"),
        P("section", "shard", None, None),
        P("section", "shard", None),
        P("shard", "section"),
    )
    out_specs = (P("shard"), P("shard", None, "section"), P("section", None))
    return jax.shard_map(local, mesh=mesh, in_specs=in_specs, out_specs=out_specs, check_vma=False)
```

```python
import jax
import jax.numpy as jnp
from jax import lax
from jax.sharding import PartitionSpec as P
from jax.experimental import pallas as pl
from jax.experimental.pallas import tpu as pltpu

SHARPNESS = 64.0
EPSILON = 1e-06
NEGATIVE = -1e30
CAPACITY = 2
GROUP = 64


def combined_all(value, axis, join):
    other = lax.ppermute(jnp.stack(value), axis, [(0, 1), (1, 0)])
    return join(value, tuple(other[place] for place in range(len(value))))


def token_scores(q_rows, blocks, cand_lens):
    logits = (
        jnp.einsum("bid,btd->bit", q_rows, blocks, preferred_element_type=jnp.float32) * SHARPNESS
    )
    in_range = jnp.arange(blocks.shape[1])[None, None, :] < cand_lens[:, None, None]
    logits = jnp.where(in_range, logits, NEGATIVE)
    top_logit = jnp.max(logits, axis=2, keepdims=True)
    expo_terms = jnp.where(in_range, jnp.exp(logits - top_logit), 0.0)
    total = jnp.sum(expo_terms, axis=2, keepdims=True)
    token_max = (top_logit[..., 0] + jnp.log(total[..., 0])) / SHARPNESS
    return (token_max, expo_terms / total)


def merge_halves(first, second):
    teach_top = jnp.maximum(first[0], second[0])
    scale_one = jnp.exp(first[0] - teach_top)
    scale_two = jnp.exp(second[0] - teach_top)
    stud_top = jnp.maximum(first[3], second[3])
    fact_one = jnp.exp(first[3] - stud_top)
    fact_two = jnp.exp(second[3] - stud_top)
    return (
        teach_top,
        first[1] * scale_one + second[1] * scale_two,
        first[2] * scale_one + second[2] * scale_two,
        stud_top,
        first[4] * fact_one + second[4] * fact_two,
    )


def pair_sum(value):
    return value + lax.ppermute(value, "section", [(0, 1), (1, 0)])


def spread_sum(value, axis, size):
    pieces = value.reshape(size, -1, value.shape[-1])
    summed = lax.all_to_all(pieces, axis, 0, 0, tiled=True).sum(axis=0)
    spread = jnp.broadcast_to(summed[None], pieces.shape)
    return lax.all_to_all(spread, axis, 0, 0, tiled=True).reshape(value.shape)


def split_three(value):
    high = lax.reduce_precision(value, exponent_bits=8, mantissa_bits=7)
    rest = value - high
    middle = lax.reduce_precision(rest, exponent_bits=8, mantissa_bits=7)
    return high, middle, rest - middle


def lane_row(width, entries):
    lane = jnp.arange(width)[None, :]
    row = jnp.zeros((entries[0].shape[0], width), jnp.float32)
    for place, entry in enumerate(entries):
        spots = entry.shape[1]
        for spot in range(spots):
            row = jnp.where(lane == place * spots + spot, entry[:, spot : spot + 1].astype(jnp.float32), row)
    return row.astype(jnp.bfloat16)[:, None, :]


def score_kernel(slot_ref, qlen_ref, len_ref, q_ref, p_ref, pt_ref, pulled_ref, stud_ref):
    group, num_tokens, _ = q_ref.shape
    pass_tokens = p_ref.shape[1]
    base = pl.program_id(0) * group
    for spot in range(group):
        slot = slot_ref[base + spot]
        limit = len_ref[slot]
        logits = (
            lax.dot_general(
                p_ref[slot], q_ref[spot], (((1,), (1,)), ((), ())), preferred_element_type=jnp.float32
            )
            * SHARPNESS
        )
        in_range = lax.broadcasted_iota(jnp.int32, (pass_tokens, num_tokens), 0) < limit
        logits = jnp.where(in_range, logits, NEGATIVE)
        top_logit = jnp.max(logits, axis=0, keepdims=True)
        expo_terms = jnp.where(in_range, jnp.exp(logits - top_logit), 0.0)
        total = jnp.sum(expo_terms, axis=0, keepdims=True)
        token_max = (top_logit + jnp.log(total)) / SHARPNESS
        weight = (expo_terms / total).astype(jnp.bfloat16)
        pulled = jnp.dot(pt_ref[slot], weight, preferred_element_type=jnp.float32)
        pulled_ref[spot] = pulled.T.astype(jnp.bfloat16)
        cols = lax.broadcasted_iota(jnp.int32, (1, num_tokens), 1)
        score = jnp.sum(jnp.where(cols < qlen_ref[base + spot], token_max, 0.0))
        stud_ref[pl.ds(spot, 1), :] = jnp.full((1, stud_ref.shape[1]), score, jnp.float32)


def owner_scores(q_rows, passages, slot_at, qlen_at, pass_len):
    slots, num_tokens, vec_dim = q_rows.shape
    held, pass_tokens, _ = passages.shape
    group = GROUP
    grid_spec = pltpu.PrefetchScalarGridSpec(
        num_scalar_prefetch=3,
        grid=(slots // group,),
        in_specs=[
            pl.BlockSpec((group, num_tokens, vec_dim), lambda i, *_: (i, 0, 0)),
            pl.BlockSpec((held, pass_tokens, vec_dim), lambda i, *_: (0, 0, 0)),
            pl.BlockSpec((held, vec_dim, pass_tokens), lambda i, *_: (0, 0, 0)),
        ],
        out_specs=[
            pl.BlockSpec((group, num_tokens, vec_dim), lambda i, *_: (i, 0, 0)),
            pl.BlockSpec((group, 128), lambda i, *_: (i, 0)),
        ],
    )
    flops = 4 * slots * num_tokens * pass_tokens * vec_dim
    moved = 2 * (2 * held * pass_tokens * vec_dim + 2 * slots * num_tokens * vec_dim)
    return pl.pallas_call(
        score_kernel,
        grid_spec=grid_spec,
        out_shape=[
            jax.ShapeDtypeStruct((slots, num_tokens, vec_dim), jnp.bfloat16),
            jax.ShapeDtypeStruct((slots, 128), jnp.float32),
        ],
        compiler_params=pltpu.CompilerParams(vmem_limit_bytes=60 * 1024 * 1024),
        cost_estimate=pl.CostEstimate(
            flops=flops, transcendentals=slots * num_tokens * pass_tokens, bytes_accessed=moved
        ),
    )(slot_at, qlen_at, pass_len, q_rows, passages, jnp.swapaxes(passages, 1, 2))


def local(hidden, proj, passages, pass_len, query_len, cand_owner, cand_slot, teacher):
    num_queries, num_tokens, feat_half = hidden.shape
    vec_dim = proj.shape[1]
    held = passages.shape[0]
    owners = lax.axis_size("shard")
    flat_h = hidden.reshape(num_queries * num_tokens, feat_half)
    partial_in = jnp.dot(flat_h, proj, preferred_element_type=jnp.float32).reshape(
        num_queries, num_tokens, vec_dim
    )
    proj_in = pair_sum(partial_in)
    inv_norm = lax.rsqrt(jnp.sum(proj_in * proj_in, axis=2, keepdims=True) + EPSILON)
    query_vecs = (proj_in * inv_norm).astype(jnp.bfloat16)
    tok_mask = jnp.arange(num_tokens)[None, :] < query_len[:, None]
    owner_ids = cand_owner.reshape(-1)
    slot_ids = cand_slot.reshape(-1)
    requests = owner_ids.shape[0]
    cand_half = requests // num_queries
    capacity = CAPACITY
    slots = owners * capacity
    onehot = (owner_ids[:, None] == jnp.arange(owners)[None, :]).astype(jnp.int32)
    rank_ids = jnp.sum((jnp.cumsum(onehot, axis=0) - onehot) * onehot, axis=1)
    buf_pos = owner_ids * capacity + rank_ids
    query_of = jnp.arange(requests) // cand_half
    pick = buf_pos[None, :] == jnp.arange(slots)[:, None]
    slot_query = jnp.any(pick[:, :, None] & (query_of[:, None] == jnp.arange(num_queries))[None], axis=1)
    q_send = jnp.einsum(
        "sq,qid->sid", slot_query.astype(jnp.bfloat16), query_vecs, preferred_element_type=jnp.float32
    ).astype(jnp.bfloat16)
    slot_meta = jnp.sum(jnp.where(pick, slot_ids[None, :], 0), axis=1).reshape(owners, capacity)
    qlen_meta = jnp.sum(jnp.where(pick, query_len[query_of][None, :], 0), axis=1).reshape(owners, capacity)
    body = capacity * num_tokens
    payload = jnp.concatenate(
        [q_send.reshape(owners, body, vec_dim), lane_row(vec_dim, (slot_meta, qlen_meta))], axis=1
    )
    recv = lax.all_to_all(payload, "shard", 0, 0, tiled=True)
    q_rows = recv[:, :body, :].reshape(slots, num_tokens, vec_dim)
    slot_at = recv[:, body, :capacity].astype(jnp.int32).reshape(slots)
    qlen_at = recv[:, body, capacity : 2 * capacity].astype(jnp.int32).reshape(slots)
    pulled, stud_rows = owner_scores(q_rows, passages, slot_at, qlen_at, pass_len)
    stud_at = stud_rows[:, 0]
    pieces = tuple(piece.reshape(owners, capacity) for piece in split_three(stud_at))
    back = jnp.concatenate(
        [pulled.reshape(owners, body, vec_dim), lane_row(vec_dim, pieces)], axis=1
    )
    got = lax.all_to_all(back, "shard", 0, 0, tiled=True)
    got_pulled = got[:, :body, :].reshape(slots, num_tokens, vec_dim)
    take = pick.T.astype(jnp.bfloat16)
    mine = jnp.einsum("rs,sid->rid", take, got_pulled, preferred_element_type=jnp.float32)
    got_meta = got[:, body, : 3 * capacity].astype(jnp.float32).reshape(owners, 3, capacity)
    got_meta = jnp.transpose(got_meta, (1, 0, 2)).reshape(3, slots)
    parts = jnp.sum(jnp.where(pick[None], got_meta[:, :, None], 0.0), axis=1)
    student = ((parts[0] + parts[1]) + parts[2]).reshape(num_queries, cand_half)
    pulled_mine = mine.reshape(num_queries, cand_half, num_tokens, vec_dim)
    teach_top = jnp.max(teacher, axis=1)
    teach_exp = jnp.exp(teacher - teach_top[:, None])
    teach_sum = jnp.sum(teach_exp, axis=1)
    teach_wsum = jnp.sum(teach_exp * (teacher - student), axis=1)
    stud_top = jnp.max(student, axis=1)
    stud_sum = jnp.sum(jnp.exp(student - stud_top[:, None]), axis=1)
    top_teach, sum_teach, wsum_teach, top_stud, sum_stud = combined_all(
        (teach_top, teach_sum, teach_wsum, stud_top, stud_sum), "section", merge_halves
    )
    lse_teach = top_teach + jnp.log(sum_teach)
    lse_stud = top_stud + jnp.log(sum_stud)
    kl_div = wsum_teach / sum_teach - lse_teach + lse_stud
    score_grad = jnp.exp(student - lse_stud[:, None]) - jnp.exp(teacher - lse_teach[:, None])
    half_grad = jnp.sum(score_grad[:, :, None, None] * pulled_mine, axis=1)
    half_grad = jnp.where(tok_mask[:, :, None], half_grad, 0.0)
    vec_grad = pair_sum(half_grad)
    cubed = inv_norm * inv_norm * inv_norm
    in_grad = inv_norm * vec_grad - cubed * proj_in * jnp.sum(
        proj_in * vec_grad, axis=2, keepdims=True
    )
    flat_in = in_grad.astype(jnp.bfloat16).reshape(num_queries * num_tokens, vec_dim)
    grad_hidden = jnp.dot(flat_in, proj.T, preferred_element_type=jnp.float32).astype(jnp.bfloat16)
    grad_hidden = grad_hidden.reshape(num_queries, num_tokens, feat_half)
    local_proj = jnp.dot(flat_h.T, flat_in, preferred_element_type=jnp.float32)
    grad_proj = spread_sum(local_proj, "shard", owners)
    return (kl_div, grad_hidden, grad_proj)


def solution(mesh):
    in_specs = (
        P("shard", None, "section"),
        P("section", None),
        P("shard", None, None),
        P("shard"),
        P("shard"),
        P("section", "shard", None, None),
        P("section", "shard", None),
        P("shard", "section"),
    )
    out_specs = (P("shard"), P("shard", None, "section"), P("section", None))
    return jax.shard_map(local, mesh=mesh, in_specs=in_specs, out_specs=out_specs, check_vma=False)
```
